128 devices in a mesh: ma: 16 (over x, z), band: 8 (over y, core).
Axes of the slice: x: 4, y: 4, z: 4, core: 2. Of those that a mesh axis runs over, the one named last changes fastest.
Arguments:
- harmonics: bfloat16 [128, 8192, 256], P(('ma', 'band')), may hold values from -6 to 6
- legendre: bfloat16 [128, 2, 8192, 512], P(('ma', 'band')), may hold values from -0.0029296875 to 0.0029296875
- m_values: int32 [128], replicated, may hold values from 1 to 8191
- cycle_cell: int32 [16384], P(('ma', 'band')), may hold values from 0 to 63, as said below
- phi_cell: int32 [16384], P(('ma', 'band')), may hold values from 3 to 123
- offsets: float32 [2, 16384], P(None, ('ma', 'band')), may hold values from 0 to 1
Outputs:
- lensed: float32 [16384, 128], P(('ma', 'band'))
The draws below stay inside these ranges and needn't reach their ends.
Inputs may be any that keep to these rules, and one draw needn't show every extreme that they name: `cycle_cell`: Band-local cycle; every point held by device (ma, band) lies in latitude band `band`. For each device and each ma index q, at most 16 of its points have cycles q * 4 to q * 4 + 3, and in every band one q receives exactly 16 points from every device of the band.
All inputs are finite; a program needn't handle non-finite values.
Results may differ from the reference program's by a relative error of at most 0.0053.
Values may be sent and summed in bfloat16 or wider, within the bound.
No kernel may reach another device: no remote copies, remote signals or barrier semaphores. Data moves between devices by JAX's collectives and lax.ppermute only.
A program may use at most 64 MiB of HBM per device.

```python
import jax
import jax.numpy as jnp
from jax import lax

L = 8192
NSIM = 64
NPHI = 128
PD = 128
RD = 4
OWNERS = 16
BANDS = 8
MTOT = 128
R = 512
RB = 64
CAP = 16
PTS = 16384


def draw_cycle_cell(key, part):
    blocks = OWNERS * BANDS
    hot_owner = jax.random.randint(jax.random.fold_in(key, 11), (BANDS,), 0, OWNERS)
    block_keys = jax.random.split(jax.random.fold_in(key, 12), blocks)

    def one_block(block_key, band_index):
        key_pick, key_order, key_cycle = jax.random.split(block_key, 3)
        picked = jax.random.permutation(key_pick, (OWNERS - 1) * CAP)[:PD - CAP] // CAP + 1
        steps_away = jnp.concatenate([jnp.zeros((CAP,), jnp.int32), picked.astype(jnp.int32)])
        steps_away = jax.random.permutation(key_order, steps_away)
        owner_index = (hot_owner[band_index] + steps_away) % OWNERS
        return owner_index * RD + jax.random.randint(key_cycle, (PD,), 0, RD)
    drawn = jax.vmap(one_block)(block_keys, jnp.arange(blocks) % BANDS)
    return drawn.reshape(-1).astype(jnp.int32)


def place_ends(values, own_key, low, largest):
    spot = [jax.random.randint(jax.random.fold_in(own_key, axis), (), 0, length) for axis, length in enumerate(values.shape)]
    longest = values.shape.index(max(values.shape))
    neighbour = spot[:longest] + [(spot[longest] + 1) % values.shape[longest]] + spot[longest + 1:]
    return values.at[tuple(spot)].set(low).at[tuple(neighbour)].set(largest)


def block_levels(rng, extent, pieces, smallest, largest):
    level, own = 1.0, jax.random.fold_in(rng, 6)
    for axis_at, blocks in pieces:
        heights = jnp.exp(jax.random.uniform(jax.random.fold_in(own, axis_at), (blocks,), jnp.float32, smallest / len(pieces), largest / len(pieces)))
        level = level * jnp.repeat(heights, extent[axis_at] // blocks).reshape([-1 if axis == axis_at else 1 for axis in range(len(extent))])
    return level


def gaussian(rng, shape, deviation, bound, cuts=(), kind=jnp.bfloat16):
    values = jax.random.normal(rng, shape, jnp.float32) * deviation
    if len(cuts) > 0:
        values = block_levels(rng, shape, cuts, -0.22, 0.18) * values
    return jnp.clip(values, min=-bound, max=bound).astype(kind)


def setup_inputs(seed: int = 0) -> dict:
    streams_of = jax.random.split(jax.random.key(seed), 7)
    harmonics = gaussian(streams_of[0], (MTOT, L, 4 * NSIM), 1.0, 6.0, ((0, 128),))
    legendre = gaussian(streams_of[1], (MTOT, 2, L, R), (4 * L * MTOT) ** -0.5, 0.0029296875, ((0, 128),))
    m_values = place_ends(jax.random.randint(streams_of[2], (MTOT,), 1, L), jax.random.fold_in(streams_of[2], 1), 1, L - 1).astype(jnp.int32)
    cycle_cell = draw_cycle_cell(jax.random.fold_in(streams_of[6], 71), 0)
    phi_cell = place_ends(jax.random.randint(streams_of[4], (PTS,), 3, NPHI - 4), jax.random.fold_in(streams_of[4], 1), 3, (NPHI - 4) - 1).astype(jnp.int32)
    offsets = jnp.clip(1.0 * jax.random.uniform(streams_of[5], (2, PTS), jnp.float32) ** block_levels(streams_of[5], (2, PTS), ((1, 128),), -0.2, 0.2), 0.0, 1.0)
    return dict(harmonics=harmonics, legendre=legendre, m_values=m_values, cycle_cell=cycle_cell, phi_cell=phi_cell, offsets=offsets)


def kernel_taps(shifts):
    return jnp.sinc(shifts) * jnp.sinc(shifts / 4.0)


def tap_weights(offset_pairs):
    tap_shift = jnp.arange(8).astype(jnp.float32) - 3.0
    across = kernel_taps(tap_shift[None, :] - offset_pairs[:, 0:1])
    beside_all = kernel_taps(tap_shift[None, :] - offset_pairs[:, 1:2])
    return (across[:, :, None] * beside_all[:, None, :]).astype(jnp.bfloat16)


def combine_parts(plus_part, minus_part):
    q_real = -(plus_part[:, 0, 0] - minus_part[:, 1, 1])
    q_imag = -(plus_part[:, 0, 1] + minus_part[:, 1, 0])
    u_real = -(plus_part[:, 1, 0] + minus_part[:, 0, 1])
    u_imag = -(plus_part[:, 1, 1] - minus_part[:, 0, 0])
    real_part = jnp.concatenate([q_real, u_real], axis=1)
    imag_part = jnp.concatenate([q_imag, u_imag], axis=1)
    return jnp.stack([real_part, imag_part], axis=1).astype(jnp.bfloat16)


def legendre_step(harm_block, table_block):
    cycle_total = table_block.shape[-1]
    evolutions = harm_block.shape[-1] // 4
    contract = (((0,), (0,)), ((), ()))
    plus_part = lax.dot_general(table_block[0], harm_block, contract, preferred_element_type=jnp.float32)
    minus_part = lax.dot_general(table_block[1], harm_block, contract, preferred_element_type=jnp.float32)
    plus_part = plus_part.reshape(cycle_total, 2, 2, evolutions)
    minus_part = minus_part.reshape(cycle_total, 2, 2, evolutions)
    return combine_parts(plus_part, minus_part)


def phase_table(m_values, cell_count, lmax_width):
    pixel_index = jnp.arange(cell_count, dtype=jnp.int32)
    period = 2 * lmax_width
    phase_turns = (m_values[None, :] * pixel_index[:, None]) % period
    angles = phase_turns.astype(jnp.float32) * (2.0 * jnp.pi / period)
    return jnp.stack([jnp.cos(angles), -jnp.sin(angles)], axis=-1).astype(jnp.bfloat16)


def reference(harmonics, legendre, m_values, cycle_cell, phi_cell, offsets):
    spectra = lax.map(lambda paired: legendre_step(paired[0], paired[1]), (harmonics, legendre))
    columns = spectra.shape[-1]
    phase_rows = phase_table(m_values, NPHI, L).astype(jnp.float32)
    cycle_blocks = spectra.reshape(MTOT, R // RD, RD, 2, columns).transpose(1, 0, 2, 3, 4)

    def cycle_block(part):
        summed = jnp.einsum("kmi,mric->rkc", phase_rows, part.astype(jnp.float32), precision=lax.Precision.HIGHEST)
        return (2.0 * summed).astype(jnp.bfloat16)

    field_rows = lax.map(cycle_block, cycle_blocks)
    band_grid = field_rows.reshape(OWNERS, BANDS, RD, NPHI, columns).transpose(1, 0, 2, 3, 4)
    band_grid = band_grid.reshape(BANDS, RB, NPHI, columns)
    padded = jnp.pad(band_grid, ((0, 0), (4, 4), (0, 0), (0, 0)))
    band_of = (jnp.arange(MTOT, dtype=jnp.int32) % BANDS).astype(jnp.int32)
    cycle_blocks_pts = cycle_cell.reshape(MTOT, PD)
    phi_blocks_pts = phi_cell.reshape(MTOT, PD)
    offset_blocks = offsets.reshape(2, MTOT, PD).transpose(1, 2, 0)

    def point_block(packed):
        band_index, cycles_here, phis_here, offsets_here = packed
        band_slab = lax.dynamic_index_in_dim(padded, band_index, 0, keepdims=False)
        tap_index = jnp.arange(8, dtype=jnp.int32)
        row_index = cycles_here[:, None] + 1 + tap_index[None, :]
        col_index = phis_here[:, None] - 3 + tap_index[None, :]
        patches = band_slab[row_index[:, :, None], col_index[:, None, :]]
        weights = tap_weights(offsets_here)
        return jnp.einsum("sab,sabc->sc", weights.astype(jnp.float32), patches.astype(jnp.float32), precision=lax.Precision.HIGHEST)

    lensed = lax.map(point_block, (band_of, cycle_blocks_pts, phi_blocks_pts, offset_blocks))
    return lensed.reshape(PTS, columns)
```

```python
import jax
import jax.numpy as jnp
from jax import lax
from jax.sharding import PartitionSpec as P

NPHI = 128
TAPS = 8


def kernel_taps(shifts):
    return jnp.sinc(shifts) * jnp.sinc(shifts / 4.0)


def combine_parts(plus_part, minus_part):
    q_real = -(plus_part[:, 0, 0] - minus_part[:, 1, 1])
    q_imag = -(plus_part[:, 0, 1] + minus_part[:, 1, 0])
    u_real = -(plus_part[:, 1, 0] + minus_part[:, 0, 1])
    u_imag = -(plus_part[:, 1, 1] - minus_part[:, 0, 0])
    real_part = jnp.concatenate([q_real, u_real], axis=1)
    imag_part = jnp.concatenate([q_imag, u_imag], axis=1)
    return jnp.stack([real_part, imag_part], axis=1).astype(jnp.bfloat16)


def phase_table(m_values, cell_count, lmax_width):
    pixel_index = jnp.arange(cell_count, dtype=jnp.int32)
    period = 2 * lmax_width
    phase_turns = m_values[None, :] * pixel_index[:, None] % period
    angles = phase_turns.astype(jnp.float32) * (2.0 * jnp.pi / period)
    return jnp.stack([jnp.cos(angles), -jnp.sin(angles)], axis=-1).astype(jnp.bfloat16)


def spread_weights(starts, weights, length):
    tap_index = jnp.arange(TAPS, dtype=jnp.int32)
    target = starts[:, None] + tap_index[None, :]
    cells = jnp.arange(length, dtype=jnp.int32)
    hits = (target[:, :, None] == cells[None, None, :]).astype(jnp.float32)
    return jnp.sum(weights[:, :, None] * hits, axis=1)


def on_device(harmonics, legendre, m_values, cycle_cell, phi_cell, offsets):
    evolutions = harmonics.shape[2] // 4
    cycle_total = legendre.shape[3]
    owner_count = lax.axis_size("ma")
    band_count = lax.axis_size("band")
    cycle_depth = cycle_total // (owner_count * band_count)
    band_rows = owner_count * cycle_depth

    both = lax.dot_general(
        legendre[0], harmonics[0], (((1,), (0,)), ((), ())), preferred_element_type=jnp.float32
    )
    spectra = combine_parts(
        both[0].reshape(cycle_total, 2, 2, evolutions),
        both[1].reshape(cycle_total, 2, 2, evolutions),
    )
    width_out = spectra.shape[2]
    by_band = spectra.reshape(owner_count, band_count, cycle_depth, 2, width_out)
    by_band = by_band.transpose(1, 3, 0, 2, 4).reshape(band_count, 2, band_rows, width_out)
    send = jnp.broadcast_to(by_band[None], (owner_count,) + by_band.shape)
    send = send.reshape(owner_count * band_count, 2, band_rows, width_out)
    received = lax.all_to_all(send, ("ma", "band"), split_axis=0, concat_axis=0, tiled=True)

    phase_rows = phase_table(m_values, NPHI, harmonics.shape[1])
    blocks = received.shape[0]
    field = jnp.dot(
        phase_rows.reshape(NPHI, blocks * 2),
        received.reshape(blocks * 2, band_rows * width_out),
        preferred_element_type=jnp.float32,
    )
    field = (2.0 * field).astype(jnp.bfloat16)

    tap_shift = jnp.arange(TAPS).astype(jnp.float32) - 3.0
    across = kernel_taps(tap_shift[None, :] - offsets[0][:, None])
    beside_all = kernel_taps(tap_shift[None, :] - offsets[1][:, None])
    cycle_weights = spread_weights(cycle_cell - 3, across, band_rows)
    phi_weights = spread_weights(phi_cell - 3, beside_all, NPHI)
    dense = (phi_weights[:, :, None] * cycle_weights[:, None, :]).astype(jnp.bfloat16)
    points = dense.shape[0]
    return jnp.dot(
        dense.reshape(points, NPHI * band_rows),
        field.reshape(NPHI * band_rows, width_out),
        preferred_element_type=jnp.float32,
    )


def solution(mesh):
    in_specs = (
        P(("ma", "band"), None, None),
        P(("ma", "band"), None, None, None),
        P(),
        P(("ma", "band")),
        P(("ma", "band")),
        P(None, ("ma", "band")),
    )
    out_specs = P(("ma", "band"), None)
    return jax.shard_map(
        on_device, mesh=mesh, in_specs=in_specs, out_specs=out_specs, check_vma=False
    )
```

```python
import jax
import jax.numpy as jnp
from jax import lax
from jax.sharding import PartitionSpec as P

NPHI = 128
TAPS = 8


def kernel_taps(shifts):
    return jnp.sinc(shifts) * jnp.sinc(shifts / 4.0)


def combine_parts(plus_part, minus_part):
    q_real = -(plus_part[:, 0, 0] - minus_part[:, 1, 1])
    q_imag = -(plus_part[:, 0, 1] + minus_part[:, 1, 0])
    u_real = -(plus_part[:, 1, 0] + minus_part[:, 0, 1])
    u_imag = -(plus_part[:, 1, 1] - minus_part[:, 0, 0])
    real_part = jnp.concatenate([q_real, u_real], axis=1)
    imag_part = jnp.concatenate([q_imag, u_imag], axis=1)
    return jnp.stack([real_part, imag_part], axis=1).astype(jnp.bfloat16)


def phase_table(m_values, cell_count, lmax_width):
    pixel_index = jnp.arange(cell_count, dtype=jnp.int32)
    period = 2 * lmax_width
    phase_turns = m_values[None, :] * pixel_index[:, None] % period
    angles = phase_turns.astype(jnp.float32) * (2.0 * jnp.pi / period)
    return jnp.stack([jnp.cos(angles), -jnp.sin(angles)], axis=-1).astype(jnp.bfloat16)


def spread_weights(starts, weights, length):
    tap_index = jnp.arange(TAPS, dtype=jnp.int32)
    target = starts[:, None] + tap_index[None, :]
    cells = jnp.arange(length, dtype=jnp.int32)
    hits = (target[:, :, None] == cells[None, None, :]).astype(jnp.float32)
    return jnp.sum(weights[:, :, None] * hits, axis=1)


def on_device(harmonics, legendre, m_values, cycle_cell, phi_cell, offsets):
    evolutions = harmonics.shape[2] // 4
    cycle_total = legendre.shape[3]
    owner_count = lax.axis_size("ma")
    band_count = lax.axis_size("band")
    cycle_depth = cycle_total // (owner_count * band_count)
    band_rows = owner_count * cycle_depth

    both = lax.dot_general(
        legendre[0], harmonics[0], (((1,), (0,)), ((), ())), preferred_element_type=jnp.float32
    )
    spectra = combine_parts(
        both[0].reshape(cycle_total, 2, 2, evolutions),
        both[1].reshape(cycle_total, 2, 2, evolutions),
    )
    width_out = spectra.shape[2]
    blocks = owner_count * band_count
    send = spectra.reshape(blocks, cycle_depth, 2, width_out).transpose(0, 2, 1, 3)
    received = lax.all_to_all(send, ("ma", "band"), split_axis=0, concat_axis=0, tiled=True)

    phase_rows = phase_table(m_values, NPHI, harmonics.shape[1])
    own = jnp.dot(
        phase_rows.reshape(NPHI, blocks * 2),
        received.reshape(blocks * 2, cycle_depth * width_out),
        preferred_element_type=jnp.float32,
    )
    own = (2.0 * own).astype(jnp.bfloat16).reshape(NPHI, cycle_depth, width_out)
    own = own.transpose(1, 0, 2)
    field = lax.all_gather(own, "ma", axis=0, tiled=True)

    tap_shift = jnp.arange(TAPS).astype(jnp.float32) - 3.0
    across = kernel_taps(tap_shift[None, :] - offsets[0][:, None])
    beside_all = kernel_taps(tap_shift[None, :] - offsets[1][:, None])
    cycle_weights = spread_weights(cycle_cell - 3, across, band_rows)
    phi_weights = spread_weights(phi_cell - 3, beside_all, NPHI)
    dense = (cycle_weights[:, :, None] * phi_weights[:, None, :]).astype(jnp.bfloat16)
    points = dense.shape[0]
    return jnp.dot(
        dense.reshape(points, band_rows * NPHI),
        field.reshape(band_rows * NPHI, width_out),
        preferred_element_type=jnp.float32,
    )


def solution(mesh):
    in_specs = (
        P(("ma", "band"), None, None),
        P(("ma", "band"), None, None, None),
        P(),
        P(("ma", "band")),
        P(("ma", "band")),
        P(None, ("ma", "band")),
    )
    out_specs = P(("ma", "band"), None)
    return jax.shard_map(
        on_device, mesh=mesh, in_specs=in_specs, out_specs=out_specs, check_vma=False
    )
```

```python
import jax
import jax.numpy as jnp
from jax import lax
from jax.sharding import PartitionSpec as P

NPHI = 128
TAPS = 8
FIELDS = 8


def kernel_taps(shifts):
    return jnp.sinc(shifts) * jnp.sinc(shifts / 4.0)


def combine_parts(plus_part, minus_part):
    q_real = -(plus_part[:, 0, 0] - minus_part[:, 1, 1])
    q_imag = -(plus_part[:, 0, 1] + minus_part[:, 1, 0])
    u_real = -(plus_part[:, 1, 0] + minus_part[:, 0, 1])
    u_imag = -(plus_part[:, 1, 1] - minus_part[:, 0, 0])
    real_part = jnp.concatenate([q_real, u_real], axis=1)
    imag_part = jnp.concatenate([q_imag, u_imag], axis=1)
    return jnp.stack([real_part, imag_part], axis=1).astype(jnp.bfloat16)


def phase_table(m_values, cell_count, lmax_width):
    pixel_index = jnp.arange(cell_count, dtype=jnp.int32)
    period = 2 * lmax_width
    phase_turns = m_values[None, :] * pixel_index[:, None] % period
    angles = phase_turns.astype(jnp.float32) * (2.0 * jnp.pi / period)
    return jnp.stack([jnp.cos(angles), -jnp.sin(angles)], axis=-1).astype(jnp.bfloat16)


def spread_weights(starts, weights, length):
    tap_index = jnp.arange(TAPS, dtype=jnp.int32)
    target = starts[:, None] + tap_index[None, :]
    cells = jnp.arange(length, dtype=jnp.int32)
    hits = (target[:, :, None] == cells[None, None, :]).astype(jnp.float32)
    return jnp.sum(weights[:, :, None] * hits, axis=1)


def split_three(x):
    hi = lax.reduce_precision(x, exponent_bits=8, mantissa_bits=7)
    rest = x - hi
    mid = lax.reduce_precision(rest, exponent_bits=8, mantissa_bits=7)
    return hi, mid, rest - mid


def on_device(harmonics, legendre, m_values, cycle_cell, phi_cell, offsets):
    evolutions = harmonics.shape[2] // 4
    cycle_total = legendre.shape[3]
    owner_count = lax.axis_size("ma")
    band_count = lax.axis_size("band")
    blocks = owner_count * band_count
    cycle_depth = cycle_total // blocks
    window = 3 * cycle_depth
    capacity = cycle_cell.shape[0] // 8
    me = lax.axis_index("ma")
    my_band = lax.axis_index("band")

    both = lax.dot_general(
        legendre[0], harmonics[0], (((1,), (0,)), ((), ())), preferred_element_type=jnp.float32
    )
    spectra = combine_parts(
        both[0].reshape(cycle_total, 2, 2, evolutions),
        both[1].reshape(cycle_total, 2, 2, evolutions),
    )
    width_out = spectra.shape[2]
    by_band = spectra.reshape(owner_count, band_count, cycle_depth, 2, width_out)
    by_band = by_band.transpose(1, 0, 2, 3, 4)
    empty = jnp.zeros((band_count, 1, cycle_depth, 2, width_out), spectra.dtype)
    padded = jnp.concatenate([empty, by_band, empty], axis=1)
    windows = jnp.stack(
        [padded[:, s : s + owner_count] for s in range(3)], axis=2
    )
    windows = windows.transpose(1, 0, 4, 2, 3, 5).reshape(blocks, 2 * window * width_out)

    owner_index = cycle_cell // cycle_depth
    one_hot = (owner_index[:, None] == jnp.arange(owner_count, dtype=jnp.int32)[None, :]).astype(
        jnp.int32
    )
    slot_index = jnp.sum((jnp.cumsum(one_hot, axis=0) - one_hot) * one_hot, axis=1)
    flat_slot = owner_index * capacity + slot_index
    placement = (
        flat_slot[:, None] == jnp.arange(owner_count * capacity, dtype=jnp.int32)[None, :]
    ).astype(jnp.bfloat16)
    table = jnp.stack(
        [cycle_cell.astype(jnp.float32), phi_cell.astype(jnp.float32)]
        + list(split_three(offsets[0]))
        + list(split_three(offsets[1])),
        axis=1,
    ).astype(jnp.bfloat16)
    payload = jnp.dot(placement.T, table, preferred_element_type=jnp.float32)
    payload = payload.astype(jnp.bfloat16).reshape(owner_count, 1, capacity * FIELDS)
    payload = jnp.broadcast_to(payload, (owner_count, band_count, capacity * FIELDS))
    send = jnp.concatenate(
        [windows, payload.reshape(blocks, capacity * FIELDS)], axis=1
    )
    received = lax.all_to_all(send, ("ma", "band"), split_axis=0, concat_axis=0, tiled=True)

    spectral_part = received[:, : 2 * window * width_out].reshape(blocks * 2, window * width_out)
    points_in = received[:, 2 * window * width_out :].reshape(
        owner_count, band_count, capacity, FIELDS
    )
    points_in = lax.dynamic_index_in_dim(points_in, my_band, axis=1, keepdims=False)
    points_in = points_in.reshape(owner_count * capacity, FIELDS).astype(jnp.float32)

    phase_rows = phase_table(m_values, NPHI, harmonics.shape[1])
    rows = jnp.dot(
        phase_rows.reshape(NPHI, blocks * 2), spectral_part, preferred_element_type=jnp.float32
    )
    rows = (2.0 * rows).astype(jnp.bfloat16)

    cycles_here = points_in[:, 0].astype(jnp.int32)
    phis_here = points_in[:, 1].astype(jnp.int32)
    offset_rows = points_in[:, 2] + (points_in[:, 3] + points_in[:, 4])
    offset_cols = points_in[:, 5] + (points_in[:, 6] + points_in[:, 7])
    tap_shift = jnp.arange(TAPS).astype(jnp.float32) - 3.0
    across = kernel_taps(tap_shift[None, :] - offset_rows[:, None])
    beside_all = kernel_taps(tap_shift[None, :] - offset_cols[:, None])
    first_row = (me - 1) * cycle_depth
    cycle_weights = spread_weights(cycles_here - 3 - first_row, across, window)
    phi_weights = spread_weights(phis_here - 3, beside_all, NPHI)
    dense = (phi_weights[:, :, None] * cycle_weights[:, None, :]).astype(jnp.bfloat16)
    values = jnp.dot(
        dense.reshape(dense.shape[0], NPHI * window),
        rows.reshape(NPHI * window, width_out),
        preferred_element_type=jnp.float32,
    )
    values = values.reshape(owner_count, capacity, width_out)
    returned = lax.all_to_all(values, "ma", split_axis=0, concat_axis=0, tiled=True)
    return jnp.take(returned.reshape(owner_count * capacity, width_out), flat_slot, axis=0)


def solution(mesh):
    in_specs = (
        P(("ma", "band"), None, None),
        P(("ma", "band"), None, None, None),
        P(),
        P(("ma", "band")),
        P(("ma", "band")),
        P(None, ("ma", "band")),
    )
    out_specs = P(("ma", "band"), None)
    return jax.shard_map(
        on_device, mesh=mesh, in_specs=in_specs, out_specs=out_specs, check_vma=False
    )
```

```python
import jax
import jax.numpy as jnp
from jax import lax
from jax.sharding import PartitionSpec as P

NPHI = 128
TAPS = 8
FIELDS = 8


def kernel_taps(shifts):
    return jnp.sinc(shifts) * jnp.sinc(shifts / 4.0)


def combine_parts(plus_part, minus_part):
    q_real = -(plus_part[:, 0, 0] - minus_part[:, 1, 1])
    q_imag = -(plus_part[:, 0, 1] + minus_part[:, 1, 0])
    u_real = -(plus_part[:, 1, 0] + minus_part[:, 0, 1])
    u_imag = -(plus_part[:, 1, 1] - minus_part[:, 0, 0])
    real_part = jnp.concatenate([q_real, u_real], axis=1)
    imag_part = jnp.concatenate([q_imag, u_imag], axis=1)
    return jnp.stack([real_part, imag_part], axis=1).astype(jnp.bfloat16)


def phase_table(m_values, cell_count, lmax_width):
    pixel_index = jnp.arange(cell_count, dtype=jnp.int32)
    period = 2 * lmax_width
    phase_turns = m_values[None, :] * pixel_index[:, None] % period
    angles = phase_turns.astype(jnp.float32) * (2.0 * jnp.pi / period)
    return jnp.stack([jnp.cos(angles), -jnp.sin(angles)], axis=-1).astype(jnp.bfloat16)


def spread_weights(starts, weights, length):
    tap_index = jnp.arange(TAPS, dtype=jnp.int32)
    target = starts[:, None] + tap_index[None, :]
    cells = jnp.arange(length, dtype=jnp.int32)
    hits = (target[:, :, None] == cells[None, None, :]).astype(jnp.float32)
    return jnp.sum(weights[:, :, None] * hits, axis=1)


def split_three(x):
    hi = lax.reduce_precision(x, exponent_bits=8, mantissa_bits=7)
    rest = x - hi
    mid = lax.reduce_precision(rest, exponent_bits=8, mantissa_bits=7)
    return hi, mid, rest - mid


def on_device(harmonics, legendre, m_values, cycle_cell, phi_cell, offsets):
    evolutions = harmonics.shape[2] // 4
    cycle_total = legendre.shape[3]
    owner_count = lax.axis_size("ma")
    band_count = lax.axis_size("band")
    blocks = owner_count * band_count
    cycle_depth = cycle_total // blocks
    window = 3 * cycle_depth
    capacity = cycle_cell.shape[0] // 8
    me = lax.axis_index("ma")
    my_band = lax.axis_index("band")

    both = lax.dot_general(
        legendre[0], harmonics[0], (((1,), (0,)), ((), ())), preferred_element_type=jnp.float32
    )
    spectra = combine_parts(
        both[0].reshape(cycle_total, 2, 2, evolutions),
        both[1].reshape(cycle_total, 2, 2, evolutions),
    )
    width_out = spectra.shape[2]
    by_band = spectra.reshape(owner_count, band_count, cycle_depth, 2, width_out)
    by_band = by_band.transpose(1, 0, 2, 3, 4)
    empty = jnp.zeros((band_count, 1, cycle_depth, 2, width_out), spectra.dtype)
    padded = jnp.concatenate([empty, by_band, empty], axis=1)
    windows = jnp.stack(
        [padded[:, s : s + owner_count] for s in range(3)], axis=2
    )
    windows = windows.transpose(1, 0, 4, 2, 3, 5).reshape(blocks, 2, window, width_out)

    owner_index = cycle_cell // cycle_depth
    one_hot = (owner_index[:, None] == jnp.arange(owner_count, dtype=jnp.int32)[None, :]).astype(
        jnp.int32
    )
    slot_index = jnp.sum((jnp.cumsum(one_hot, axis=0) - one_hot) * one_hot, axis=1)
    flat_slot = owner_index * capacity + slot_index
    placement = (
        flat_slot[:, None] == jnp.arange(owner_count * capacity, dtype=jnp.int32)[None, :]
    ).astype(jnp.bfloat16)
    table = jnp.stack(
        [cycle_cell.astype(jnp.float32), phi_cell.astype(jnp.float32)]
        + list(split_three(offsets[0]))
        + list(split_three(offsets[1])),
        axis=1,
    ).astype(jnp.bfloat16)
    payload = jnp.dot(placement.T, table, preferred_element_type=jnp.float32)
    payload = payload.astype(jnp.bfloat16).reshape(owner_count, 1, 1, 1, capacity * FIELDS)
    payload = jnp.broadcast_to(payload, (owner_count, band_count, 1, 1, capacity * FIELDS))
    payload = payload.reshape(blocks, 1, 1, capacity * FIELDS)
    payload = jnp.concatenate([payload, jnp.zeros_like(payload)], axis=1)
    send = jnp.concatenate([windows, payload], axis=2)
    received = lax.all_to_all(send, ("ma", "band"), split_axis=0, concat_axis=0, tiled=True)

    points_in = received[:, 0, window].reshape(owner_count, band_count, capacity, FIELDS)
    points_in = lax.dynamic_index_in_dim(points_in, my_band, axis=1, keepdims=False)
    points_in = points_in.reshape(owner_count * capacity, FIELDS).astype(jnp.float32)

    phase_rows = phase_table(m_values, NPHI, harmonics.shape[1])
    rows = jnp.einsum(
        "kgi,gitc->tkc", phase_rows, received[:, :, :window], preferred_element_type=jnp.float32
    )
    rows = (2.0 * rows).astype(jnp.bfloat16)

    cycles_here = points_in[:, 0].astype(jnp.int32)
    phis_here = points_in[:, 1].astype(jnp.int32)
    offset_rows = points_in[:, 2] + (points_in[:, 3] + points_in[:, 4])
    offset_cols = points_in[:, 5] + (points_in[:, 6] + points_in[:, 7])
    tap_shift = jnp.arange(TAPS).astype(jnp.float32) - 3.0
    across = kernel_taps(tap_shift[None, :] - offset_rows[:, None])
    beside_all = kernel_taps(tap_shift[None, :] - offset_cols[:, None])
    first_row = (me - 1) * cycle_depth
    cycle_weights = spread_weights(cycles_here - 3 - first_row, across, window)
    phi_weights = spread_weights(phis_here - 3, beside_all, NPHI)
    dense = (cycle_weights[:, :, None] * phi_weights[:, None, :]).astype(jnp.bfloat16)
    values = jnp.dot(
        dense.reshape(dense.shape[0], window * NPHI),
        rows.reshape(window * NPHI, width_out),
        preferred_element_type=jnp.float32,
    )
    values = values.reshape(owner_count, capacity, width_out)
    returned = lax.all_to_all(values, "ma", split_axis=0, concat_axis=0, tiled=True)
    return jnp.take(returned.reshape(owner_count * capacity, width_out), flat_slot, axis=0)


def solution(mesh):
    in_specs = (
        P(("ma", "band"), None, None),
        P(("ma", "band"), None, None, None),
        P(),
        P(("ma", "band")),
        P(("ma", "band")),
        P(None, ("ma", "band")),
    )
    out_specs = P(("ma", "band"), None)
    return jax.shard_map(
        on_device, mesh=mesh, in_specs=in_specs, out_specs=out_specs, check_vma=False
    )
```

```python
import jax
import jax.numpy as jnp
from jax import lax
from jax.sharding import PartitionSpec as P

NPHI = 128
TAPS = 8
FIELDS = 8


def kernel_taps(shifts):
    return jnp.sinc(shifts) * jnp.sinc(shifts / 4.0)


def combine_parts(plus_part, minus_part):
    q_real = -(plus_part[:, 0, 0] - minus_part[:, 1, 1])
    q_imag = -(plus_part[:, 0, 1] + minus_part[:, 1, 0])
    u_real = -(plus_part[:, 1, 0] + minus_part[:, 0, 1])
    u_imag = -(plus_part[:, 1, 1] - minus_part[:, 0, 0])
    real_part = jnp.concatenate([q_real, u_real], axis=1)
    imag_part = jnp.concatenate([q_imag, u_imag], axis=1)
    return jnp.stack([real_part, imag_part], axis=1).astype(jnp.bfloat16)


def phase_table(m_values, cell_count, lmax_width):
    pixel_index = jnp.arange(cell_count, dtype=jnp.int32)
    period = 2 * lmax_width
    phase_turns = m_values[None, :] * pixel_index[:, None] % period
    angles = phase_turns.astype(jnp.float32) * (2.0 * jnp.pi / period)
    return jnp.stack([jnp.cos(angles), -jnp.sin(angles)], axis=-1).astype(jnp.bfloat16)


def spread_weights(starts, weights, length):
    tap_index = jnp.arange(TAPS, dtype=jnp.int32)
    target = starts[:, None] + tap_index[None, :]
    cells = jnp.arange(length, dtype=jnp.int32)
    hits = (target[:, :, None] == cells[None, None, :]).astype(jnp.float32)
    return jnp.sum(weights[:, :, None] * hits, axis=1)


def split_three(x):
    hi = lax.reduce_precision(x, exponent_bits=8, mantissa_bits=7)
    rest = x - hi
    mid = lax.reduce_precision(rest, exponent_bits=8, mantissa_bits=7)
    return hi, mid, rest - mid


def on_device(harmonics, legendre, m_values, cycle_cell, phi_cell, offsets):
    evolutions = harmonics.shape[2] // 4
    cycle_total = legendre.shape[3]
    owner_count = lax.axis_size("ma")
    band_count = lax.axis_size("band")
    blocks = owner_count * band_count
    cycle_depth = cycle_total // blocks
    window = 3 * cycle_depth
    capacity = cycle_cell.shape[0] // 8
    me = lax.axis_index("ma")
    my_band = lax.axis_index("band")

    both = lax.dot_general(
        legendre[0], harmonics[0], (((1,), (0,)), ((), ())), preferred_element_type=jnp.float32
    )
    spectra = combine_parts(
        both[0].reshape(cycle_total, 2, 2, evolutions),
        both[1].reshape(cycle_total, 2, 2, evolutions),
    )
    width_out = spectra.shape[2]
    by_band = spectra.reshape(owner_count, band_count, cycle_depth, 2, width_out)
    by_band = by_band.transpose(1, 0, 2, 3, 4)
    empty = jnp.zeros((band_count, 1, cycle_depth, 2, width_out), spectra.dtype)
    padded = jnp.concatenate([empty, by_band, empty], axis=1)
    windows = jnp.stack(
        [padded[:, s : s + owner_count] for s in range(3)], axis=2
    )
    windows = windows.transpose(1, 0, 4, 2, 3, 5).reshape(blocks, 2, window, width_out)

    owner_index = cycle_cell // cycle_depth
    one_hot = (owner_index[:, None] == jnp.arange(owner_count, dtype=jnp.int32)[None, :]).astype(
        jnp.int32
    )
    slot_index = jnp.sum((jnp.cumsum(one_hot, axis=0) - one_hot) * one_hot, axis=1)
    flat_slot = owner_index * capacity + slot_index
    placement = (
        flat_slot[:, None] == jnp.arange(owner_count * capacity, dtype=jnp.int32)[None, :]
    ).astype(jnp.bfloat16)
    table = jnp.stack(
        [cycle_cell.astype(jnp.float32), phi_cell.astype(jnp.float32)]
        + list(split_three(offsets[0]))
        + list(split_three(offsets[1])),
        axis=1,
    ).astype(jnp.bfloat16)
    payload = jnp.dot(placement.T, table, preferred_element_type=jnp.float32)
    payload = payload.astype(jnp.bfloat16).reshape(owner_count, 1, 1, 1, capacity * FIELDS)
    payload = jnp.broadcast_to(payload, (owner_count, band_count, 1, 1, capacity * FIELDS))
    payload = payload.reshape(blocks, 1, 1, capacity * FIELDS)
    payload = jnp.concatenate([payload, jnp.zeros_like(payload)], axis=1)
    send = jnp.concatenate([windows, payload], axis=2)
    send = send.reshape((owner_count, band_count) + send.shape[1:])
    staged = lax.all_to_all(send, "band", split_axis=1, concat_axis=1, tiled=True)
    received = lax.all_to_all(staged, "ma", split_axis=0, concat_axis=0, tiled=True)
    received = received.reshape((blocks,) + received.shape[2:])

    points_in = received[:, 0, window].reshape(owner_count, band_count, capacity, FIELDS)
    points_in = lax.dynamic_index_in_dim(points_in, my_band, axis=1, keepdims=False)
    points_in = points_in.reshape(owner_count * capacity, FIELDS).astype(jnp.float32)

    phase_rows = phase_table(m_values, NPHI, harmonics.shape[1])
    rows = jnp.einsum(
        "kgi,gitc->tkc", phase_rows, received[:, :, :window], preferred_element_type=jnp.float32
    )
    rows = (2.0 * rows).astype(jnp.bfloat16)

    cycles_here = points_in[:, 0].astype(jnp.int32)
    phis_here = points_in[:, 1].astype(jnp.int32)
    offset_rows = points_in[:, 2] + (points_in[:, 3] + points_in[:, 4])
    offset_cols = points_in[:, 5] + (points_in[:, 6] + points_in[:, 7])
    tap_shift = jnp.arange(TAPS).astype(jnp.float32) - 3.0
    across = kernel_taps(tap_shift[None, :] - offset_rows[:, None])
    beside_all = kernel_taps(tap_shift[None, :] - offset_cols[:, None])
    first_row = (me - 1) * cycle_depth
    cycle_weights = spread_weights(cycles_here - 3 - first_row, across, window)
    phi_weights = spread_weights(phis_here - 3, beside_all, NPHI)
    dense = (cycle_weights[:, :, None] * phi_weights[:, None, :]).astype(jnp.bfloat16)
    values = jnp.dot(
        dense.reshape(dense.shape[0], window * NPHI),
        rows.reshape(window * NPHI, width_out),
        preferred_element_type=jnp.float32,
    )
    values = values.reshape(owner_count, capacity, width_out)
    returned = lax.all_to_all(values, "ma", split_axis=0, concat_axis=0, tiled=True)
    return jnp.take(returned.reshape(owner_count * capacity, width_out), flat_slot, axis=0)


def solution(mesh):
    in_specs = (
        P(("ma", "band"), None, None),
        P(("ma", "band"), None, None, None),
        P(),
        P(("ma", "band")),
        P(("ma", "band")),
        P(None, ("ma", "band")),
    )
    out_specs = P(("ma", "band"), None)
    return jax.shard_map(
        on_device, mesh=mesh, in_specs=in_specs, out_specs=out_specs, check_vma=False
    )
```

```python
import jax
import jax.numpy as jnp
from jax import lax
from jax.experimental import pallas as pl
from jax.experimental.pallas import tpu as pltpu
from jax.sharding import PartitionSpec as P

NPHI = 128
TAPS = 8
FIELDS = 8
DEPTH_TILE = 1024


def synthesis_kernel(table_ref, harm_ref, out_ref):
    @pl.when(pl.program_id(0) == 0)
    def _():
        out_ref[...] = jnp.zeros_like(out_ref)

    harm = harm_ref[...]
    contract = (((0,), (0,)), ((), ()))
    for part in range(2):
        out_ref[part] += lax.dot_general(
            harm, table_ref[part], contract, preferred_element_type=jnp.float32
        )


def synthesize(harmonics, legendre):
    _, depth, columns = harmonics.shape
    cycles = legendre.shape[3]
    steps = depth // DEPTH_TILE
    return pl.pallas_call(
        synthesis_kernel,
        grid=(steps,),
        in_specs=[
            pl.BlockSpec((None, 2, DEPTH_TILE, cycles), lambda k: (0, 0, k, 0)),
            pl.BlockSpec((None, DEPTH_TILE, columns), lambda k: (0, k, 0)),
        ],
        out_specs=pl.BlockSpec((2, columns, cycles), lambda k: (0, 0, 0)),
        out_shape=jax.ShapeDtypeStruct((2, columns, cycles), jnp.float32),
        compiler_params=pltpu.CompilerParams(dimension_semantics=("arbitrary",)),
        cost_estimate=pl.CostEstimate(
            flops=4 * depth * cycles * columns,
            transcendentals=0,
            bytes_accessed=2 * (2 * depth * cycles + depth * columns) + 8 * cycles * columns,
        ),
    )(legendre, harmonics)


def kernel_taps(shifts):
    return jnp.sinc(shifts) * jnp.sinc(shifts / 4.0)


def combine_parts(plus_part, minus_part):
    q_real = -(plus_part[:, 0, 0] - minus_part[:, 1, 1])
    q_imag = -(plus_part[:, 0, 1] + minus_part[:, 1, 0])
    u_real = -(plus_part[:, 1, 0] + minus_part[:, 0, 1])
    u_imag = -(plus_part[:, 1, 1] - minus_part[:, 0, 0])
    real_part = jnp.concatenate([q_real, u_real], axis=1)
    imag_part = jnp.concatenate([q_imag, u_imag], axis=1)
    return jnp.stack([real_part, imag_part], axis=1).astype(jnp.bfloat16)


def phase_table(m_values, cell_count, lmax_width):
    pixel_index = jnp.arange(cell_count, dtype=jnp.int32)
    period = 2 * lmax_width
    phase_turns = m_values[None, :] * pixel_index[:, None] % period
    angles = phase_turns.astype(jnp.float32) * (2.0 * jnp.pi / period)
    return jnp.stack([jnp.cos(angles), -jnp.sin(angles)], axis=-1).astype(jnp.bfloat16)


def spread_weights(starts, weights, length):
    tap_index = jnp.arange(TAPS, dtype=jnp.int32)
    target = starts[:, None] + tap_index[None, :]
    cells = jnp.arange(length, dtype=jnp.int32)
    hits = (target[:, :, None] == cells[None, None, :]).astype(jnp.float32)
    return jnp.sum(weights[:, :, None] * hits, axis=1)


def split_three(x):
    hi = lax.reduce_precision(x, exponent_bits=8, mantissa_bits=7)
    rest = x - hi
    mid = lax.reduce_precision(rest, exponent_bits=8, mantissa_bits=7)
    return hi, mid, rest - mid


def on_device(harmonics, legendre, m_values, cycle_cell, phi_cell, offsets):
    evolutions = harmonics.shape[2] // 4
    cycle_total = legendre.shape[3]
    owner_count = lax.axis_size("ma")
    band_count = lax.axis_size("band")
    blocks = owner_count * band_count
    cycle_depth = cycle_total // blocks
    window = 3 * cycle_depth
    capacity = cycle_cell.shape[0] // 8
    me = lax.axis_index("ma")
    my_band = lax.axis_index("band")

    both = synthesize(harmonics, legendre)
    plus_part = both[0].reshape(2, 2, evolutions, cycle_total)
    minus_part = both[1].reshape(2, 2, evolutions, cycle_total)
    q_real = -(plus_part[0, 0] - minus_part[1, 1])
    q_imag = -(plus_part[0, 1] + minus_part[1, 0])
    u_real = -(plus_part[1, 0] + minus_part[0, 1])
    u_imag = -(plus_part[1, 1] - minus_part[0, 0])
    real_part = jnp.concatenate([q_real, u_real], axis=0)
    imag_part = jnp.concatenate([q_imag, u_imag], axis=0)
    spectra = jnp.stack([real_part, imag_part], axis=0).astype(jnp.bfloat16).transpose(0, 2, 1)
    width_out = spectra.shape[2]
    by_band = spectra.reshape(2, owner_count, band_count, cycle_depth, width_out)
    by_band = by_band.transpose(2, 1, 0, 3, 4)
    empty = jnp.zeros((band_count, 1, 2, cycle_depth, width_out), spectra.dtype)
    padded = jnp.concatenate([empty, by_band, empty], axis=1)
    windows = jnp.stack(
        [padded[:, s : s + owner_count] for s in range(3)], axis=3
    )
    windows = windows.transpose(1, 0, 2, 3, 4, 5).reshape(blocks, 2, window, width_out)

    owner_index = cycle_cell // cycle_depth
    one_hot = (owner_index[:, None] == jnp.arange(owner_count, dtype=jnp.int32)[None, :]).astype(
        jnp.int32
    )
    slot_index = jnp.sum((jnp.cumsum(one_hot, axis=0) - one_hot) * one_hot, axis=1)
    flat_slot = owner_index * capacity + slot_index
    placement = (
        flat_slot[:, None] == jnp.arange(owner_count * capacity, dtype=jnp.int32)[None, :]
    ).astype(jnp.bfloat16)
    table = jnp.stack(
        [cycle_cell.astype(jnp.float32), phi_cell.astype(jnp.float32)]
        + list(split_three(offsets[0]))
        + list(split_three(offsets[1])),
        axis=1,
    ).astype(jnp.bfloat16)
    payload = jnp.dot(placement.T, table, preferred_element_type=jnp.float32)
    payload = payload.astype(jnp.bfloat16).reshape(owner_count, 1, 1, 1, capacity * FIELDS)
    payload = jnp.broadcast_to(payload, (owner_count, band_count, 1, 1, capacity * FIELDS))
    payload = payload.reshape(blocks, 1, 1, capacity * FIELDS)
    payload = jnp.concatenate([payload, jnp.zeros_like(payload)], axis=1)
    send = jnp.concatenate([windows, payload], axis=2)
    received = lax.all_to_all(send, ("ma", "band"), split_axis=0, concat_axis=0, tiled=True)

    points_in = received[:, 0, window].reshape(owner_count, band_count, capacity, FIELDS)
    points_in = lax.dynamic_index_in_dim(points_in, my_band, axis=1, keepdims=False)
    points_in = points_in.reshape(owner_count * capacity, FIELDS).astype(jnp.float32)

    phase_rows = phase_table(m_values, NPHI, harmonics.shape[1])
    rows = jnp.einsum(
        "kgi,gitc->tkc", phase_rows, received[:, :, :window], preferred_element_type=jnp.float32
    )
    rows = (2.0 * rows).astype(jnp.bfloat16)

    cycles_here = points_in[:, 0].astype(jnp.int32)
    phis_here = points_in[:, 1].astype(jnp.int32)
    offset_rows = points_in[:, 2] + (points_in[:, 3] + points_in[:, 4])
    offset_cols = points_in[:, 5] + (points_in[:, 6] + points_in[:, 7])
    tap_shift = jnp.arange(TAPS).astype(jnp.float32) - 3.0
    across = kernel_taps(tap_shift[None, :] - offset_rows[:, None])
    beside_all = kernel_taps(tap_shift[None, :] - offset_cols[:, None])
    first_row = (me - 1) * cycle_depth
    cycle_weights = spread_weights(cycles_here - 3 - first_row, across, window)
    phi_weights = spread_weights(phis_here - 3, beside_all, NPHI)
    dense = (cycle_weights[:, :, None] * phi_weights[:, None, :]).astype(jnp.bfloat16)
    values = jnp.dot(
        dense.reshape(dense.shape[0], window * NPHI),
        rows.reshape(window * NPHI, width_out),
        preferred_element_type=jnp.float32,
    )
    values = values.reshape(owner_count, capacity, width_out)
    returned = lax.all_to_all(values, "ma", split_axis=0, concat_axis=0, tiled=True)
    return jnp.take(returned.reshape(owner_count * capacity, width_out), flat_slot, axis=0)


def solution(mesh):
    in_specs = (
        P(("ma", "band"), None, None),
        P(("ma", "band"), None, None, None),
        P(),
        P(("ma", "band")),
        P(("ma", "band")),
        P(None, ("ma", "band")),
    )
    out_specs = P(("ma", "band"), None)
    return jax.shard_map(
        on_device, mesh=mesh, in_specs=in_specs, out_specs=out_specs, check_vma=False
    )
```

```python
import jax
import jax.numpy as jnp
from jax import lax
from jax.sharding import PartitionSpec as P

NPHI = 128
TAPS = 8
FIELDS = 8


def kernel_taps(shifts):
    return jnp.sinc(shifts) * jnp.sinc(shifts / 4.0)


def combine_parts(plus_part, minus_part):
    q_real = -(plus_part[:, 0, 0] - minus_part[:, 1, 1])
    q_imag = -(plus_part[:, 0, 1] + minus_part[:, 1, 0])
    u_real = -(plus_part[:, 1, 0] + minus_part[:, 0, 1])
    u_imag = -(plus_part[:, 1, 1] - minus_part[:, 0, 0])
    real_part = jnp.concatenate([q_real, u_real], axis=1)
    imag_part = jnp.concatenate([q_imag, u_imag], axis=1)
    return jnp.stack([real_part, imag_part], axis=1).astype(jnp.bfloat16)


def phase_table(m_values, cell_count, lmax_width):
    pixel_index = jnp.arange(cell_count, dtype=jnp.int32)
    period = 2 * lmax_width
    phase_turns = m_values[None, :] * pixel_index[:, None] % period
    angles = phase_turns.astype(jnp.float32) * (2.0 * jnp.pi / period)
    return jnp.stack([jnp.cos(angles), -jnp.sin(angles)], axis=-1).astype(jnp.bfloat16)


def spread_weights(starts, weights, length):
    tap_index = jnp.arange(TAPS, dtype=jnp.int32)
    target = starts[:, None] + tap_index[None, :]
    cells = jnp.arange(length, dtype=jnp.int32)
    hits = (target[:, :, None] == cells[None, None, :]).astype(jnp.float32)
    return jnp.sum(weights[:, :, None] * hits, axis=1)


def split_three(x):
    hi = lax.reduce_precision(x, exponent_bits=8, mantissa_bits=7)
    rest = x - hi
    mid = lax.reduce_precision(rest, exponent_bits=8, mantissa_bits=7)
    return hi, mid, rest - mid


def on_device(harmonics, legendre, m_values, cycle_cell, phi_cell, offsets):
    evolutions = harmonics.shape[2] // 4
    cycle_total = legendre.shape[3]
    owner_count = lax.axis_size("ma")
    band_count = lax.axis_size("band")
    blocks = owner_count * band_count
    cycle_depth = cycle_total // blocks
    window = 3 * cycle_depth
    lead = 1
    capacity = cycle_cell.shape[0] // 8
    me = lax.axis_index("ma")
    my_band = lax.axis_index("band")

    both = lax.dot_general(
        legendre[0], harmonics[0], (((1,), (0,)), ((), ())), preferred_element_type=jnp.float32
    )
    spectra = combine_parts(
        both[0].reshape(cycle_total, 2, 2, evolutions),
        both[1].reshape(cycle_total, 2, 2, evolutions),
    )
    width_out = spectra.shape[2]
    by_band = spectra.reshape(owner_count, band_count, cycle_depth, 2, width_out)
    by_band = by_band.transpose(1, 0, 2, 3, 4)
    empty = jnp.zeros((band_count, 1, cycle_depth, 2, width_out), spectra.dtype)
    padded = jnp.concatenate([empty, by_band, empty], axis=1)
    windows = jnp.stack(
        [padded[:, s : s + owner_count] for s in range(3)], axis=2
    )
    windows = windows.transpose(1, 0, 4, 2, 3, 5).reshape(blocks, 2, window, width_out)
    windows = windows[:, :, lead:]

    owner_index = cycle_cell // cycle_depth
    one_hot = (owner_index[:, None] == jnp.arange(owner_count, dtype=jnp.int32)[None, :]).astype(
        jnp.int32
    )
    slot_index = jnp.sum((jnp.cumsum(one_hot, axis=0) - one_hot) * one_hot, axis=1)
    flat_slot = owner_index * capacity + slot_index
    placement = (
        flat_slot[:, None] == jnp.arange(owner_count * capacity, dtype=jnp.int32)[None, :]
    ).astype(jnp.bfloat16)
    table = jnp.stack(
        [cycle_cell.astype(jnp.float32), phi_cell.astype(jnp.float32)]
        + list(split_three(offsets[0]))
        + list(split_three(offsets[1])),
        axis=1,
    ).astype(jnp.bfloat16)
    payload = jnp.dot(placement.T, table, preferred_element_type=jnp.float32)
    payload = payload.astype(jnp.bfloat16).reshape(owner_count, 1, 1, 1, capacity * FIELDS)
    payload = jnp.broadcast_to(payload, (owner_count, band_count, 1, 1, capacity * FIELDS))
    payload = payload.reshape(blocks, 1, 1, capacity * FIELDS)
    payload = jnp.concatenate([payload, jnp.zeros_like(payload)], axis=1)
    send = jnp.concatenate([windows, payload], axis=2)
    received = lax.all_to_all(send, ("ma", "band"), split_axis=0, concat_axis=0, tiled=True)

    points_in = received[:, 0, window - lead].reshape(owner_count, band_count, capacity, FIELDS)
    points_in = lax.dynamic_index_in_dim(points_in, my_band, axis=1, keepdims=False)
    points_in = points_in.reshape(owner_count * capacity, FIELDS).astype(jnp.float32)

    phase_rows = phase_table(m_values, NPHI, harmonics.shape[1])
    rows = jnp.einsum(
        "kgi,gitc->tkc", phase_rows, received, preferred_element_type=jnp.float32
    )
    rows = (2.0 * rows).astype(jnp.bfloat16)

    cycles_here = points_in[:, 0].astype(jnp.int32)
    phis_here = points_in[:, 1].astype(jnp.int32)
    offset_rows = points_in[:, 2] + (points_in[:, 3] + points_in[:, 4])
    offset_cols = points_in[:, 5] + (points_in[:, 6] + points_in[:, 7])
    tap_shift = jnp.arange(TAPS).astype(jnp.float32) - 3.0
    across = kernel_taps(tap_shift[None, :] - offset_rows[:, None])
    beside_all = kernel_taps(tap_shift[None, :] - offset_cols[:, None])
    first_row = (me - 1) * cycle_depth + lead
    cycle_weights = spread_weights(cycles_here - 3 - first_row, across, window)
    phi_weights = spread_weights(phis_here - 3, beside_all, NPHI)
    dense = (cycle_weights[:, :, None] * phi_weights[:, None, :]).astype(jnp.bfloat16)
    values = jnp.dot(
        dense.reshape(dense.shape[0], window * NPHI),
        rows.reshape(window * NPHI, width_out),
        preferred_element_type=jnp.float32,
    )
    values = values.reshape(owner_count, capacity, width_out)
    returned = lax.all_to_all(values, "ma", split_axis=0, concat_axis=0, tiled=True)
    return jnp.take(returned.reshape(owner_count * capacity, width_out), flat_slot, axis=0)


def solution(mesh):
    in_specs = (
        P(("ma", "band"), None, None),
        P(("ma", "band"), None, None, None),
        P(),
        P(("ma", "band")),
        P(("ma", "band")),
        P(None, ("ma", "band")),
    )
    out_specs = P(("ma", "band"), None)
    return jax.shard_map(
        on_device, mesh=mesh, in_specs=in_specs, out_specs=out_specs, check_vma=False
    )
```

```python
import jax
import jax.numpy as jnp
from jax import lax
from jax.sharding import PartitionSpec as P

NPHI = 128
TAPS = 8
FIELDS = 8


def kernel_taps(shifts):
    return jnp.sinc(shifts) * jnp.sinc(shifts / 4.0)


def combine_parts(plus_part, minus_part):
    q_real = -(plus_part[:, 0, 0] - minus_part[:, 1, 1])
    q_imag = -(plus_part[:, 0, 1] + minus_part[:, 1, 0])
    u_real = -(plus_part[:, 1, 0] + minus_part[:, 0, 1])
    u_imag = -(plus_part[:, 1, 1] - minus_part[:, 0, 0])
    real_part = jnp.concatenate([q_real, u_real], axis=1)
    imag_part = jnp.concatenate([q_imag, u_imag], axis=1)
    return jnp.stack([real_part, imag_part], axis=1).astype(jnp.bfloat16)


def phase_table(m_values, cell_count, lmax_width):
    pixel_index = jnp.arange(cell_count, dtype=jnp.int32)
    period = 2 * lmax_width
    phase_turns = m_values[None, :] * pixel_index[:, None] % period
    angles = phase_turns.astype(jnp.float32) * (2.0 * jnp.pi / period)
    return jnp.stack([jnp.cos(angles), -jnp.sin(angles)], axis=-1).astype(jnp.bfloat16)


def spread_weights(starts, weights, length):
    cells = jnp.arange(length, dtype=jnp.int32)[None, :] - starts[:, None]
    spread = jnp.zeros(cells.shape, weights.dtype)
    for tap in range(TAPS):
        spread = spread + jnp.where(cells == tap, weights[:, tap : tap + 1], 0.0)
    return spread


def split_three(x):
    hi = lax.reduce_precision(x, exponent_bits=8, mantissa_bits=7)
    rest = x - hi
    mid = lax.reduce_precision(rest, exponent_bits=8, mantissa_bits=7)
    return hi, mid, rest - mid


def on_device(harmonics, legendre, m_values, cycle_cell, phi_cell, offsets):
    evolutions = harmonics.shape[2] // 4
    cycle_total = legendre.shape[3]
    owner_count = lax.axis_size("ma")
    band_count = lax.axis_size("band")
    blocks = owner_count * band_count
    cycle_depth = cycle_total // blocks
    window = 3 * cycle_depth
    lead = 1
    capacity = cycle_cell.shape[0] // 8
    me = lax.axis_index("ma")
    my_band = lax.axis_index("band")

    both = lax.dot_general(
        legendre[0], harmonics[0], (((1,), (0,)), ((), ())), preferred_element_type=jnp.float32
    )
    spectra = combine_parts(
        both[0].reshape(cycle_total, 2, 2, evolutions),
        both[1].reshape(cycle_total, 2, 2, evolutions),
    )
    width_out = spectra.shape[2]
    by_band = spectra.reshape(owner_count, band_count, cycle_depth, 2, width_out)
    by_band = by_band.transpose(1, 0, 2, 3, 4)
    empty = jnp.zeros((band_count, 1, cycle_depth, 2, width_out), spectra.dtype)
    padded = jnp.concatenate([empty, by_band, empty], axis=1)
    windows = jnp.stack(
        [padded[:, s : s + owner_count] for s in range(3)], axis=2
    )
    windows = windows.transpose(1, 0, 4, 2, 3, 5).reshape(blocks, 2, window, width_out)
    windows = windows[:, :, lead:]

    owner_index = cycle_cell // cycle_depth
    one_hot = (owner_index[:, None] == jnp.arange(owner_count, dtype=jnp.int32)[None, :]).astype(
        jnp.int32
    )
    slot_index = jnp.sum((jnp.cumsum(one_hot, axis=0) - one_hot) * one_hot, axis=1)
    flat_slot = owner_index * capacity + slot_index
    placement = (
        flat_slot[:, None] == jnp.arange(owner_count * capacity, dtype=jnp.int32)[None, :]
    ).astype(jnp.bfloat16)
    table = jnp.stack(
        [cycle_cell.astype(jnp.float32), phi_cell.astype(jnp.float32)]
        + list(split_three(offsets[0]))
        + list(split_three(offsets[1])),
        axis=1,
    ).astype(jnp.bfloat16)
    payload = jnp.dot(placement.T, table, preferred_element_type=jnp.float32)
    payload = payload.astype(jnp.bfloat16).reshape(owner_count, 1, 1, 1, capacity * FIELDS)
    payload = jnp.broadcast_to(payload, (owner_count, band_count, 1, 1, capacity * FIELDS))
    payload = payload.reshape(blocks, 1, 1, capacity * FIELDS)
    payload = jnp.concatenate([payload, jnp.zeros_like(payload)], axis=1)
    send = jnp.concatenate([windows, payload], axis=2)
    received = lax.all_to_all(send, ("ma", "band"), split_axis=0, concat_axis=0, tiled=True)

    points_in = received[:, 0, window - lead].reshape(owner_count, band_count, capacity, FIELDS)
    points_in = lax.dynamic_index_in_dim(points_in, my_band, axis=1, keepdims=False)
    points_in = points_in.reshape(owner_count * capacity, FIELDS).astype(jnp.float32)

    phase_rows = phase_table(m_values, NPHI, harmonics.shape[1])
    rows = jnp.einsum(
        "kgi,gitc->tkc", phase_rows, received, preferred_element_type=jnp.float32
    )
    rows = (2.0 * rows).astype(jnp.bfloat16)

    cycles_here = points_in[:, 0].astype(jnp.int32)
    phis_here = points_in[:, 1].astype(jnp.int32)
    offset_rows = points_in[:, 2] + (points_in[:, 3] + points_in[:, 4])
    offset_cols = points_in[:, 5] + (points_in[:, 6] + points_in[:, 7])
    tap_shift = jnp.arange(TAPS).astype(jnp.float32) - 3.0
    across = kernel_taps(tap_shift[None, :] - offset_rows[:, None])
    beside_all = kernel_taps(tap_shift[None, :] - offset_cols[:, None])
    first_row = (me - 1) * cycle_depth + lead
    cycle_weights = spread_weights(cycles_here - 3 - first_row, across, window)
    phi_weights = spread_weights(phis_here - 3, beside_all, NPHI)
    dense = (cycle_weights[:, :, None] * phi_weights[:, None, :]).astype(jnp.bfloat16)
    values = lax.dot_general(
        dense, rows, (((1, 2), (0, 1)), ((), ())), preferred_element_type=jnp.float32
    )
    values = values.reshape(owner_count, capacity, width_out)
    returned = lax.all_to_all(values, "ma", split_axis=0, concat_axis=0, tiled=True)
    return jnp.take(returned.reshape(owner_count * capacity, width_out), flat_slot, axis=0, mode="clip")


def solution(mesh):
    in_specs = (
        P(("ma", "band"), None, None),
        P(("ma", "band"), None, None, None),
        P(),
        P(("ma", "band")),
        P(("ma", "band")),
        P(None, ("ma", "band")),
    )
    out_specs = P(("ma", "band"), None)
    return jax.shard_map(
        on_device, mesh=mesh, in_specs=in_specs, out_specs=out_specs, check_vma=False
    )
```

```python
import jax
import jax.numpy as jnp
from jax import lax
from jax.experimental.layout import Layout, with_layout_constraint
from jax.sharding import PartitionSpec as P

NPHI = 128
TAPS = 8
FIELDS = 8


def kernel_taps(shifts):
    return jnp.sinc(shifts) * jnp.sinc(shifts / 4.0)


def combine_parts(plus_part, minus_part):
    q_real = -(plus_part[:, 0, 0] - minus_part[:, 1, 1])
    q_imag = -(plus_part[:, 0, 1] + minus_part[:, 1, 0])
    u_real = -(plus_part[:, 1, 0] + minus_part[:, 0, 1])
    u_imag = -(plus_part[:, 1, 1] - minus_part[:, 0, 0])
    real_part = jnp.concatenate([q_real, u_real], axis=1)
    imag_part = jnp.concatenate([q_imag, u_imag], axis=1)
    return jnp.stack([real_part, imag_part], axis=1).astype(jnp.bfloat16)


def phase_table(m_values, cell_count, lmax_width):
    pixel_index = jnp.arange(cell_count, dtype=jnp.int32)
    period = 2 * lmax_width
    phase_turns = m_values[None, :] * pixel_index[:, None] % period
    angles = phase_turns.astype(jnp.float32) * (2.0 * jnp.pi / period)
    return jnp.stack([jnp.cos(angles), -jnp.sin(angles)], axis=-1).astype(jnp.bfloat16)


def spread_weights(starts, weights, length):
    cells = jnp.arange(length, dtype=jnp.int32)[None, :] - starts[:, None]
    spread = jnp.zeros(cells.shape, weights.dtype)
    for tap in range(TAPS):
        spread = spread + jnp.where(cells == tap, weights[:, tap : tap + 1], 0.0)
    return spread


def split_three(x):
    hi = lax.reduce_precision(x, exponent_bits=8, mantissa_bits=7)
    rest = x - hi
    mid = lax.reduce_precision(rest, exponent_bits=8, mantissa_bits=7)
    return hi, mid, rest - mid


def on_device(harmonics, legendre, m_values, cycle_cell, phi_cell, offsets):
    evolutions = harmonics.shape[2] // 4
    cycle_total = legendre.shape[3]
    owner_count = lax.axis_size("ma")
    band_count = lax.axis_size("band")
    blocks = owner_count * band_count
    cycle_depth = cycle_total // blocks
    window = 3 * cycle_depth
    lead = 1
    capacity = cycle_cell.shape[0] // 8
    me = lax.axis_index("ma")
    my_band = lax.axis_index("band")

    both = lax.dot_general(
        legendre[0], harmonics[0], (((1,), (0,)), ((), ())), preferred_element_type=jnp.float32
    )
    spectra = combine_parts(
        both[0].reshape(cycle_total, 2, 2, evolutions),
        both[1].reshape(cycle_total, 2, 2, evolutions),
    )
    width_out = spectra.shape[2]
    by_band = spectra.reshape(owner_count, band_count, cycle_depth, 2, width_out)
    by_band = by_band.transpose(1, 0, 2, 3, 4)
    empty = jnp.zeros((band_count, 1, cycle_depth, 2, width_out), spectra.dtype)
    padded = jnp.concatenate([empty, by_band, empty], axis=1)
    windows = jnp.stack(
        [padded[:, s : s + owner_count] for s in range(3)], axis=2
    )
    windows = windows.transpose(1, 0, 4, 2, 3, 5).reshape(blocks, 2, window, width_out)
    windows = windows[:, :, lead:]

    owner_index = cycle_cell // cycle_depth
    one_hot = (owner_index[:, None] == jnp.arange(owner_count, dtype=jnp.int32)[None, :]).astype(
        jnp.int32
    )
    slot_index = jnp.sum((jnp.cumsum(one_hot, axis=0) - one_hot) * one_hot, axis=1)
    flat_slot = owner_index * capacity + slot_index
    placement = (
        flat_slot[:, None] == jnp.arange(owner_count * capacity, dtype=jnp.int32)[None, :]
    ).astype(jnp.bfloat16)
    table = jnp.stack(
        [cycle_cell.astype(jnp.float32), phi_cell.astype(jnp.float32)]
        + list(split_three(offsets[0]))
        + list(split_three(offsets[1])),
        axis=1,
    ).astype(jnp.bfloat16)
    payload = jnp.dot(placement.T, table, preferred_element_type=jnp.float32)
    payload = payload.astype(jnp.bfloat16).reshape(owner_count, 1, 1, 1, capacity * FIELDS)
    payload = jnp.broadcast_to(payload, (owner_count, band_count, 1, 1, capacity * FIELDS))
    payload = payload.reshape(blocks, 1, 1, capacity * FIELDS)
    payload = jnp.concatenate([payload, jnp.zeros_like(payload)], axis=1)
    send = jnp.concatenate([windows, payload], axis=2)
    send = with_layout_constraint(send, Layout(major_to_minor=(0, 2, 1, 3)))
    received = lax.all_to_all(send, ("ma", "band"), split_axis=0, concat_axis=0, tiled=True)

    points_in = received[:, 0, window - lead].reshape(owner_count, band_count, capacity, FIELDS)
    points_in = lax.dynamic_index_in_dim(points_in, my_band, axis=1, keepdims=False)
    points_in = points_in.reshape(owner_count * capacity, FIELDS).astype(jnp.float32)

    phase_rows = phase_table(m_values, NPHI, harmonics.shape[1])
    rows = jnp.einsum(
        "kgi,gitc->tkc", phase_rows, received, preferred_element_type=jnp.float32
    )
    rows = (2.0 * rows).astype(jnp.bfloat16)

    cycles_here = points_in[:, 0].astype(jnp.int32)
    phis_here = points_in[:, 1].astype(jnp.int32)
    offset_rows = points_in[:, 2] + (points_in[:, 3] + points_in[:, 4])
    offset_cols = points_in[:, 5] + (points_in[:, 6] + points_in[:, 7])
    tap_shift = jnp.arange(TAPS).astype(jnp.float32) - 3.0
    across = kernel_taps(tap_shift[None, :] - offset_rows[:, None])
    beside_all = kernel_taps(tap_shift[None, :] - offset_cols[:, None])
    first_row = (me - 1) * cycle_depth + lead
    cycle_weights = spread_weights(cycles_here - 3 - first_row, across, window)
    phi_weights = spread_weights(phis_here - 3, beside_all, NPHI)
    dense = (cycle_weights[:, :, None] * phi_weights[:, None, :]).astype(jnp.bfloat16)
    values = lax.dot_general(
        dense, rows, (((1, 2), (0, 1)), ((), ())), preferred_element_type=jnp.float32
    )
    values = values.reshape(owner_count, capacity, width_out)
    returned = lax.all_to_all(values, "ma", split_axis=0, concat_axis=0, tiled=True)
    return jnp.take(returned.reshape(owner_count * capacity, width_out), flat_slot, axis=0, mode="clip")


def solution(mesh):
    in_specs = (
        P(("ma", "band"), None, None),
        P(("ma", "band"), None, None, None),
        P(),
        P(("ma", "band")),
        P(("ma", "band")),
        P(None, ("ma", "band")),
    )
    out_specs = P(("ma", "band"), None)
    return jax.shard_map(
        on_device, mesh=mesh, in_specs=in_specs, out_specs=out_specs, check_vma=False
    )
```

```python
import jax
import jax.numpy as jnp
from jax import lax
from jax.sharding import PartitionSpec as P

NPHI = 128
TAPS = 8
FIELDS = 8


def kernel_taps(shifts):
    return jnp.sinc(shifts) * jnp.sinc(shifts / 4.0)


def combine_parts(plus_part, minus_part):
    q_real = -(plus_part[:, 0, 0] - minus_part[:, 1, 1])
    q_imag = -(plus_part[:, 0, 1] + minus_part[:, 1, 0])
    u_real = -(plus_part[:, 1, 0] + minus_part[:, 0, 1])
    u_imag = -(plus_part[:, 1, 1] - minus_part[:, 0, 0])
    real_part = jnp.concatenate([q_real, u_real], axis=1)
    imag_part = jnp.concatenate([q_imag, u_imag], axis=1)
    return jnp.stack([real_part, imag_part], axis=1).astype(jnp.bfloat16)


def phase_table(m_values, cell_count, lmax_width):
    pixel_index = jnp.arange(cell_count, dtype=jnp.int32)
    period = 2 * lmax_width
    phase_turns = m_values[None, :] * pixel_index[:, None] % period
    angles = phase_turns.astype(jnp.float32) * (2.0 * jnp.pi / period)
    return jnp.stack([jnp.cos(angles), -jnp.sin(angles)], axis=-1).astype(jnp.bfloat16)


def spread_weights(starts, weights, length):
    cells = jnp.arange(length, dtype=jnp.int32)[None, :] - starts[:, None]
    spread = jnp.zeros(cells.shape, weights.dtype)
    for tap in range(TAPS):
        spread = spread + jnp.where(cells == tap, weights[:, tap : tap + 1], 0.0)
    return spread


def split_three(x):
    hi = lax.reduce_precision(x, exponent_bits=8, mantissa_bits=7)
    rest = x - hi
    mid = lax.reduce_precision(rest, exponent_bits=8, mantissa_bits=7)
    return hi, mid, rest - mid


def on_device(harmonics, legendre, m_values, cycle_cell, phi_cell, offsets):
    evolutions = harmonics.shape[2] // 4
    cycle_total = legendre.shape[3]
    owner_count = lax.axis_size("ma")
    band_count = lax.axis_size("band")
    blocks = owner_count * band_count
    cycle_depth = cycle_total // blocks
    window = 3 * cycle_depth
    lead = 1
    capacity = cycle_cell.shape[0] // 8
    me = lax.axis_index("ma")
    my_band = lax.axis_index("band")

    both = lax.dot_general(
        legendre[0], harmonics[0], (((1,), (0,)), ((), ())), preferred_element_type=jnp.float32
    )
    spectra = combine_parts(
        both[0].reshape(cycle_total, 2, 2, evolutions),
        both[1].reshape(cycle_total, 2, 2, evolutions),
    )
    width_out = spectra.shape[2]
    by_band = spectra.reshape(owner_count, band_count, cycle_depth, 2, width_out)
    by_band = by_band.transpose(1, 0, 2, 3, 4)
    empty = jnp.zeros((band_count, 1, cycle_depth, 2, width_out), spectra.dtype)
    padded = jnp.concatenate([empty, by_band, empty], axis=1)
    windows = jnp.stack(
        [padded[:, s : s + owner_count] for s in range(3)], axis=2
    )
    windows = windows.transpose(1, 0, 4, 2, 3, 5).reshape(blocks, 2, window, width_out)
    windows = windows[:, :, lead:]

    owner_index = cycle_cell // cycle_depth
    one_hot = (owner_index[:, None] == jnp.arange(owner_count, dtype=jnp.int32)[None, :]).astype(
        jnp.int32
    )
    slot_index = jnp.sum((jnp.cumsum(one_hot, axis=0) - one_hot) * one_hot, axis=1)
    flat_slot = owner_index * capacity + slot_index
    placement = (
        flat_slot[:, None] == jnp.arange(owner_count * capacity, dtype=jnp.int32)[None, :]
    ).astype(jnp.bfloat16)
    table = jnp.stack(
        [cycle_cell.astype(jnp.float32), phi_cell.astype(jnp.float32)]
        + list(split_three(offsets[0]))
        + list(split_three(offsets[1])),
        axis=1,
    ).astype(jnp.bfloat16)
    payload = jnp.dot(placement.T, table, preferred_element_type=jnp.float32)
    payload = payload.astype(jnp.bfloat16).reshape(owner_count, 1, 1, 1, capacity * FIELDS)
    payload = jnp.broadcast_to(payload, (owner_count, band_count, 1, 1, capacity * FIELDS))
    payload = payload.reshape(blocks, 1, 1, capacity * FIELDS)
    payload = jnp.concatenate([payload, jnp.zeros_like(payload)], axis=1)
    send = jnp.concatenate([windows, payload], axis=2)
    received = lax.all_to_all(send, ("ma", "band"), split_axis=0, concat_axis=0, tiled=True)

    points_in = received[:, 0, window - lead].reshape(owner_count, band_count, capacity, FIELDS)
    points_in = lax.dynamic_index_in_dim(points_in, my_band, axis=1, keepdims=False)
    points_in = points_in.reshape(owner_count * capacity, FIELDS).astype(jnp.float32)

    phase_rows = phase_table(m_values, NPHI, harmonics.shape[1])
    rows = jnp.einsum(
        "kgi,gitc->tkc", phase_rows, received, preferred_element_type=jnp.float32
    )
    rows = (2.0 * rows).astype(jnp.bfloat16)

    cycles_here = points_in[:, 0].astype(jnp.int32)
    phis_here = points_in[:, 1].astype(jnp.int32)
    offset_rows = points_in[:, 2] + (points_in[:, 3] + points_in[:, 4])
    offset_cols = points_in[:, 5] + (points_in[:, 6] + points_in[:, 7])
    tap_shift = jnp.arange(TAPS).astype(jnp.float32) - 3.0
    across = kernel_taps(tap_shift[None, :] - offset_rows[:, None])
    beside_all = kernel_taps(tap_shift[None, :] - offset_cols[:, None])
    first_row = (me - 1) * cycle_depth + lead
    cycle_weights = spread_weights(cycles_here - 3 - first_row, across, window)
    phi_weights = spread_weights(phis_here - 3, beside_all, NPHI)
    dense = (cycle_weights[:, :, None] * phi_weights[:, None, :]).astype(jnp.bfloat16)
    values = lax.dot_general(
        dense, rows, (((1, 2), (0, 1)), ((), ())), preferred_element_type=jnp.float32
    )
    values = values.reshape(owner_count, capacity, width_out)
    returned = lax.all_to_all(values, "ma", split_axis=0, concat_axis=0, tiled=True)
    pick = (
        flat_slot[:, None] == jnp.arange(owner_count * capacity, dtype=jnp.int32)[None, :]
    ).astype(jnp.float32)
    return jnp.dot(
        pick,
        returned.reshape(owner_count * capacity, width_out),
        precision=lax.Precision.HIGHEST,
    )


def solution(mesh):
    in_specs = (
        P(("ma", "band"), None, None),
        P(("ma", "band"), None, None, None),
        P(),
        P(("ma", "band")),
        P(("ma", "band")),
        P(None, ("ma", "band")),
    )
    out_specs = P(("ma", "band"), None)
    return jax.shard_map(
        on_device, mesh=mesh, in_specs=in_specs, out_specs=out_specs, check_vma=False
    )
```

```python
import jax
import jax.numpy as jnp
from jax import lax
from jax.experimental.layout import Layout, with_layout_constraint
from jax.sharding import PartitionSpec as P

NPHI = 128
TAPS = 8
FIELDS = 8


def kernel_taps(shifts):
    return jnp.sinc(shifts) * jnp.sinc(shifts / 4.0)


def combine_parts(plus_part, minus_part):
    q_real = -(plus_part[:, 0, 0] - minus_part[:, 1, 1])
    q_imag = -(plus_part[:, 0, 1] + minus_part[:, 1, 0])
    u_real = -(plus_part[:, 1, 0] + minus_part[:, 0, 1])
    u_imag = -(plus_part[:, 1, 1] - minus_part[:, 0, 0])
    real_part = jnp.concatenate([q_real, u_real], axis=1)
    imag_part = jnp.concatenate([q_imag, u_imag], axis=1)
    return jnp.stack([real_part, imag_part], axis=1).astype(jnp.bfloat16)


def phase_table(m_values, cell_count, lmax_width):
    pixel_index = jnp.arange(cell_count, dtype=jnp.int32)
    period = 2 * lmax_width
    phase_turns = m_values[None, :] * pixel_index[:, None] % period
    angles = phase_turns.astype(jnp.float32) * (2.0 * jnp.pi / period)
    return jnp.stack([jnp.cos(angles), -jnp.sin(angles)], axis=-1).astype(jnp.bfloat16)


def spread_weights(starts, weights, length):
    cells = jnp.arange(length, dtype=jnp.int32)[None, :] - starts[:, None]
    spread = jnp.zeros(cells.shape, weights.dtype)
    for tap in range(TAPS):
        spread = spread + jnp.where(cells == tap, weights[:, tap : tap + 1], 0.0)
    return spread


def split_three(x):
    hi = lax.reduce_precision(x, exponent_bits=8, mantissa_bits=7)
    rest = x - hi
    mid = lax.reduce_precision(rest, exponent_bits=8, mantissa_bits=7)
    return hi, mid, rest - mid


def on_device(harmonics, legendre, m_values, cycle_cell, phi_cell, offsets):
    evolutions = harmonics.shape[2] // 4
    cycle_total = legendre.shape[3]
    owner_count = lax.axis_size("ma")
    band_count = lax.axis_size("band")
    blocks = owner_count * band_count
    cycle_depth = cycle_total // blocks
    window = 3 * cycle_depth
    lead = 1
    capacity = cycle_cell.shape[0] // 8
    me = lax.axis_index("ma")
    my_band = lax.axis_index("band")

    both = lax.dot_general(
        legendre[0], harmonics[0], (((1,), (0,)), ((), ())), preferred_element_type=jnp.float32
    )
    both = with_layout_constraint(both, Layout(major_to_minor=(0, 1, 2)))
    spectra = combine_parts(
        both[0].reshape(cycle_total, 2, 2, evolutions),
        both[1].reshape(cycle_total, 2, 2, evolutions),
    )
    width_out = spectra.shape[2]
    by_band = spectra.reshape(owner_count, band_count, cycle_depth, 2, width_out)
    by_band = by_band.transpose(1, 0, 2, 3, 4)
    empty = jnp.zeros((band_count, 1, cycle_depth, 2, width_out), spectra.dtype)
    padded = jnp.concatenate([empty, by_band, empty], axis=1)
    windows = jnp.stack(
        [padded[:, s : s + owner_count] for s in range(3)], axis=2
    )
    windows = windows.transpose(1, 0, 4, 2, 3, 5).reshape(blocks, 2, window, width_out)
    windows = windows[:, :, lead:]

    owner_index = cycle_cell // cycle_depth
    one_hot = (owner_index[:, None] == jnp.arange(owner_count, dtype=jnp.int32)[None, :]).astype(
        jnp.int32
    )
    slot_index = jnp.sum((jnp.cumsum(one_hot, axis=0) - one_hot) * one_hot, axis=1)
    flat_slot = owner_index * capacity + slot_index
    placement = (
        flat_slot[:, None] == jnp.arange(owner_count * capacity, dtype=jnp.int32)[None, :]
    ).astype(jnp.bfloat16)
    table = jnp.stack(
        [cycle_cell.astype(jnp.float32), phi_cell.astype(jnp.float32)]
        + list(split_three(offsets[0]))
        + list(split_three(offsets[1])),
        axis=1,
    ).astype(jnp.bfloat16)
    payload = jnp.dot(placement.T, table, preferred_element_type=jnp.float32)
    payload = payload.astype(jnp.bfloat16).reshape(owner_count, 1, 1, 1, capacity * FIELDS)
    payload = jnp.broadcast_to(payload, (owner_count, band_count, 1, 1, capacity * FIELDS))
    payload = payload.reshape(blocks, 1, 1, capacity * FIELDS)
    payload = jnp.concatenate([payload, jnp.zeros_like(payload)], axis=1)
    send = jnp.concatenate([windows, payload], axis=2)
    received = lax.all_to_all(send, ("ma", "band"), split_axis=0, concat_axis=0, tiled=True)

    points_in = received[:, 0, window - lead].reshape(owner_count, band_count, capacity, FIELDS)
    points_in = lax.dynamic_index_in_dim(points_in, my_band, axis=1, keepdims=False)
    points_in = points_in.reshape(owner_count * capacity, FIELDS).astype(jnp.float32)

    phase_rows = phase_table(m_values, NPHI, harmonics.shape[1])
    rows = jnp.einsum(
        "kgi,gitc->tkc", phase_rows, received, preferred_element_type=jnp.float32
    )
    rows = (2.0 * rows).astype(jnp.bfloat16)

    cycles_here = points_in[:, 0].astype(jnp.int32)
    phis_here = points_in[:, 1].astype(jnp.int32)
    offset_rows = points_in[:, 2] + (points_in[:, 3] + points_in[:, 4])
    offset_cols = points_in[:, 5] + (points_in[:, 6] + points_in[:, 7])
    tap_shift = jnp.arange(TAPS).astype(jnp.float32) - 3.0
    across = kernel_taps(tap_shift[None, :] - offset_rows[:, None])
    beside_all = kernel_taps(tap_shift[None, :] - offset_cols[:, None])
    first_row = (me - 1) * cycle_depth + lead
    cycle_weights = spread_weights(cycles_here - 3 - first_row, across, window)
    phi_weights = spread_weights(phis_here - 3, beside_all, NPHI)
    dense = (cycle_weights[:, :, None] * phi_weights[:, None, :]).astype(jnp.bfloat16)
    values = lax.dot_general(
        dense, rows, (((1, 2), (0, 1)), ((), ())), preferred_element_type=jnp.float32
    )
    values = values.reshape(owner_count, capacity, width_out)
    returned = lax.all_to_all(values, "ma", split_axis=0, concat_axis=0, tiled=True)
    pick = (
        flat_slot[:, None] == jnp.arange(owner_count * capacity, dtype=jnp.int32)[None, :]
    ).astype(jnp.float32)
    return jnp.dot(
        pick,
        returned.reshape(owner_count * capacity, width_out),
        precision=lax.Precision.HIGHEST,
    )


def solution(mesh):
    in_specs = (
        P(("ma", "band"), None, None),
        P(("ma", "band"), None, None, None),
        P(),
        P(("ma", "band")),
        P(("ma", "band")),
        P(None, ("ma", "band")),
    )
    out_specs = P(("ma", "band"), None)
    return jax.shard_map(
        on_device, mesh=mesh, in_specs=in_specs, out_specs=out_specs, check_vma=False
    )
```

```python
import jax
import jax.numpy as jnp
from jax import lax
from jax.sharding import PartitionSpec as P

NPHI = 128
TAPS = 8
FIELDS = 8


def kernel_taps(shifts):
    return jnp.sinc(shifts) * jnp.sinc(shifts / 4.0)


def combine_parts(plus_part, minus_part):
    q_real = -(plus_part[:, 0, 0] - minus_part[:, 1, 1])
    q_imag = -(plus_part[:, 0, 1] + minus_part[:, 1, 0])
    u_real = -(plus_part[:, 1, 0] + minus_part[:, 0, 1])
    u_imag = -(plus_part[:, 1, 1] - minus_part[:, 0, 0])
    real_part = jnp.concatenate([q_real, u_real], axis=1)
    imag_part = jnp.concatenate([q_imag, u_imag], axis=1)
    return jnp.stack([real_part, imag_part], axis=1).astype(jnp.bfloat16)


def phase_table(m_values, cell_count, lmax_width):
    pixel_index = jnp.arange(cell_count, dtype=jnp.int32)
    period = 2 * lmax_width
    phase_turns = m_values[None, :] * pixel_index[:, None] % period
    angles = phase_turns.astype(jnp.float32) * (2.0 * jnp.pi / period)
    return jnp.stack([jnp.cos(angles), -jnp.sin(angles)], axis=-1).astype(jnp.bfloat16)


def spread_weights(starts, weights, length):
    cells = jnp.arange(length, dtype=jnp.int32)[None, :] - starts[:, None]
    spread = jnp.zeros(cells.shape, weights.dtype)
    for tap in range(TAPS):
        spread = spread + jnp.where(cells == tap, weights[:, tap : tap + 1], 0.0)
    return spread


def split_three(x):
    hi = lax.reduce_precision(x, exponent_bits=8, mantissa_bits=7)
    rest = x - hi
    mid = lax.reduce_precision(rest, exponent_bits=8, mantissa_bits=7)
    return hi, mid, rest - mid


def on_device(harmonics, legendre, m_values, cycle_cell, phi_cell, offsets):
    evolutions = harmonics.shape[2] // 4
    cycle_total = legendre.shape[3]
    owner_count = lax.axis_size("ma")
    band_count = lax.axis_size("band")
    blocks = owner_count * band_count
    cycle_depth = cycle_total // blocks
    window = 3 * cycle_depth
    lead = 1
    capacity = cycle_cell.shape[0] // 8
    me = lax.axis_index("ma")
    my_band = lax.axis_index("band")

    both = lax.dot_general(
        legendre[0], harmonics[0], (((1,), (0,)), ((), ())), preferred_element_type=jnp.float32
    )
    spectra = combine_parts(
        both[0].reshape(cycle_total, 2, 2, evolutions),
        both[1].reshape(cycle_total, 2, 2, evolutions),
    )
    width_out = spectra.shape[2]
    by_band = spectra.reshape(owner_count, band_count, cycle_depth, 2, width_out)
    by_band = by_band.transpose(1, 0, 2, 3, 4)
    empty = jnp.zeros((band_count, 1, cycle_depth, 2, width_out), spectra.dtype)
    padded = jnp.concatenate([empty, by_band, empty], axis=1)
    windows = jnp.stack(
        [padded[:, s : s + owner_count] for s in range(3)], axis=2
    )
    windows = windows.transpose(1, 0, 4, 2, 3, 5).reshape(blocks, 2, window, width_out)
    windows = windows[:, :, lead:]

    owner_index = cycle_cell // cycle_depth
    one_hot = (owner_index[:, None] == jnp.arange(owner_count, dtype=jnp.int32)[None, :]).astype(
        jnp.int32
    )
    slot_index = jnp.sum((jnp.cumsum(one_hot, axis=0) - one_hot) * one_hot, axis=1)
    flat_slot = owner_index * capacity + slot_index
    placement = (
        flat_slot[:, None] == jnp.arange(owner_count * capacity, dtype=jnp.int32)[None, :]
    ).astype(jnp.bfloat16)
    table = jnp.stack(
        [cycle_cell.astype(jnp.float32), phi_cell.astype(jnp.float32)]
        + list(split_three(offsets[0]))
        + list(split_three(offsets[1])),
        axis=1,
    ).astype(jnp.bfloat16)
    payload = jnp.dot(table.T, placement, preferred_element_type=jnp.float32)
    payload = payload.astype(jnp.bfloat16).reshape(FIELDS, owner_count, capacity)
    payload = payload.transpose(1, 0, 2).reshape(owner_count, 1, 1, 1, capacity * FIELDS)
    payload = jnp.broadcast_to(payload, (owner_count, band_count, 1, 1, capacity * FIELDS))
    payload = payload.reshape(blocks, 1, 1, capacity * FIELDS)
    payload = jnp.concatenate([payload, jnp.zeros_like(payload)], axis=1)
    send = jnp.concatenate([windows, payload], axis=2)
    received = lax.all_to_all(send, ("ma", "band"), split_axis=0, concat_axis=0, tiled=True)

    points_in = received[:, 0, window - lead].reshape(owner_count, band_count, capacity * FIELDS)
    points_in = lax.dynamic_index_in_dim(points_in, my_band, axis=1, keepdims=False)
    points_in = points_in.reshape(owner_count, FIELDS, capacity).transpose(1, 0, 2)
    points_in = points_in.reshape(FIELDS, owner_count * capacity).astype(jnp.float32)

    phase_rows = phase_table(m_values, NPHI, harmonics.shape[1])
    rows = jnp.einsum(
        "kgi,gitc->tkc", phase_rows, received, preferred_element_type=jnp.float32
    )
    rows = (2.0 * rows).astype(jnp.bfloat16)

    cycles_here = points_in[0].astype(jnp.int32)
    phis_here = points_in[1].astype(jnp.int32)
    offset_rows = points_in[2] + (points_in[3] + points_in[4])
    offset_cols = points_in[5] + (points_in[6] + points_in[7])
    tap_shift = jnp.arange(TAPS).astype(jnp.float32) - 3.0
    across = kernel_taps(tap_shift[None, :] - offset_rows[:, None])
    beside_all = kernel_taps(tap_shift[None, :] - offset_cols[:, None])
    first_row = (me - 1) * cycle_depth + lead
    cycle_weights = spread_weights(cycles_here - 3 - first_row, across, window)
    phi_weights = spread_weights(phis_here - 3, beside_all, NPHI)
    dense = (cycle_weights[:, :, None] * phi_weights[:, None, :]).astype(jnp.bfloat16)
    values = lax.dot_general(
        dense, rows, (((1, 2), (0, 1)), ((), ())), preferred_element_type=jnp.float32
    )
    values = values.reshape(owner_count, capacity, width_out)
    returned = lax.all_to_all(values, "ma", split_axis=0, concat_axis=0, tiled=True)
    pick = (
        flat_slot[:, None] == jnp.arange(owner_count * capacity, dtype=jnp.int32)[None, :]
    ).astype(jnp.float32)
    return jnp.dot(
        pick,
        returned.reshape(owner_count * capacity, width_out),
        precision=lax.Precision.HIGHEST,
    )


def solution(mesh):
    in_specs = (
        P(("ma", "band"), None, None),
        P(("ma", "band"), None, None, None),
        P(),
        P(("ma", "band")),
        P(("ma", "band")),
        P(None, ("ma", "band")),
    )
    out_specs = P(("ma", "band"), None)
    return jax.shard_map(
        on_device, mesh=mesh, in_specs=in_specs, out_specs=out_specs, check_vma=False
    )
```

```python
import jax
import jax.numpy as jnp
from jax import lax
from jax.experimental.layout import Layout, with_layout_constraint
from jax.sharding import PartitionSpec as P

NPHI = 128
TAPS = 8
FIELDS = 8


def kernel_taps(shifts):
    return jnp.sinc(shifts) * jnp.sinc(shifts / 4.0)


def combine_parts(plus_part, minus_part):
    q_real = -(plus_part[:, 0, 0] - minus_part[:, 1, 1])
    q_imag = -(plus_part[:, 0, 1] + minus_part[:, 1, 0])
    u_real = -(plus_part[:, 1, 0] + minus_part[:, 0, 1])
    u_imag = -(plus_part[:, 1, 1] - minus_part[:, 0, 0])
    real_part = jnp.concatenate([q_real, u_real], axis=1)
    imag_part = jnp.concatenate([q_imag, u_imag], axis=1)
    return jnp.stack([real_part, imag_part], axis=1).astype(jnp.bfloat16)


def phase_table(m_values, cell_count, lmax_width):
    pixel_index = jnp.arange(cell_count, dtype=jnp.int32)
    period = 2 * lmax_width
    phase_turns = m_values[None, :] * pixel_index[:, None] % period
    angles = phase_turns.astype(jnp.float32) * (2.0 * jnp.pi / period)
    return jnp.stack([jnp.cos(angles), -jnp.sin(angles)], axis=-1).astype(jnp.bfloat16)


def spread_weights(starts, weights, length):
    cells = jnp.arange(length, dtype=jnp.int32)[None, :] - starts[:, None]
    spread = jnp.zeros(cells.shape, weights.dtype)
    for tap in range(TAPS):
        spread = spread + jnp.where(cells == tap, weights[:, tap : tap + 1], 0.0)
    return spread


def split_three(x):
    hi = lax.reduce_precision(x, exponent_bits=8, mantissa_bits=7)
    rest = x - hi
    mid = lax.reduce_precision(rest, exponent_bits=8, mantissa_bits=7)
    return hi, mid, rest - mid


def on_device(harmonics, legendre, m_values, cycle_cell, phi_cell, offsets):
    evolutions = harmonics.shape[2] // 4
    cycle_total = legendre.shape[3]
    owner_count = lax.axis_size("ma")
    band_count = lax.axis_size("band")
    blocks = owner_count * band_count
    cycle_depth = cycle_total // blocks
    window = 3 * cycle_depth
    lead = 1
    capacity = cycle_cell.shape[0] // 8
    me = lax.axis_index("ma")
    my_band = lax.axis_index("band")

    both = lax.dot_general(
        legendre[0], harmonics[0], (((1,), (0,)), ((), ())), preferred_element_type=jnp.float32
    )
    both = with_layout_constraint(both, Layout(major_to_minor=(0, 1, 2)))
    spectra = combine_parts(
        both[0].reshape(cycle_total, 2, 2, evolutions),
        both[1].reshape(cycle_total, 2, 2, evolutions),
    )
    width_out = spectra.shape[2]
    by_band = spectra.reshape(owner_count, band_count, cycle_depth, 2, width_out)
    by_band = by_band.transpose(1, 0, 2, 3, 4)
    empty = jnp.zeros((band_count, 1, cycle_depth, 2, width_out), spectra.dtype)
    padded = jnp.concatenate([empty, by_band, empty], axis=1)
    windows = jnp.stack(
        [padded[:, s : s + owner_count] for s in range(3)], axis=2
    )
    windows = windows.transpose(1, 0, 4, 2, 3, 5).reshape(blocks, 2, window, width_out)
    windows = windows[:, :, lead:]

    owner_index = cycle_cell // cycle_depth
    one_hot = (owner_index[:, None] == jnp.arange(owner_count, dtype=jnp.int32)[None, :]).astype(
        jnp.int32
    )
    slot_index = jnp.sum((jnp.cumsum(one_hot, axis=0) - one_hot) * one_hot, axis=1)
    flat_slot = owner_index * capacity + slot_index
    placement = (
        flat_slot[:, None] == jnp.arange(owner_count * capacity, dtype=jnp.int32)[None, :]
    ).astype(jnp.bfloat16)
    table = jnp.stack(
        [cycle_cell.astype(jnp.float32), phi_cell.astype(jnp.float32)]
        + list(split_three(offsets[0]))
        + list(split_three(offsets[1])),
        axis=1,
    ).astype(jnp.bfloat16)
    payload = jnp.dot(table.T, placement, preferred_element_type=jnp.float32)
    payload = payload.astype(jnp.bfloat16).reshape(FIELDS, owner_count, capacity)
    payload = payload.transpose(1, 0, 2).reshape(owner_count, 1, 1, 1, capacity * FIELDS)
    payload = jnp.broadcast_to(payload, (owner_count, band_count, 1, 1, capacity * FIELDS))
    payload = payload.reshape(blocks, 1, 1, capacity * FIELDS)
    payload = jnp.concatenate([payload, jnp.zeros_like(payload)], axis=1)
    send = jnp.concatenate([windows, payload], axis=2)
    received = lax.all_to_all(send, ("ma", "band"), split_axis=0, concat_axis=0, tiled=True)

    points_in = received[:, 0, window - lead].reshape(owner_count, band_count, capacity * FIELDS)
    points_in = lax.dynamic_index_in_dim(points_in, my_band, axis=1, keepdims=False)
    points_in = points_in.reshape(owner_count, FIELDS, capacity).transpose(1, 0, 2)
    points_in = points_in.reshape(FIELDS, owner_count * capacity).astype(jnp.float32)

    phase_rows = phase_table(m_values, NPHI, harmonics.shape[1])
    rows = jnp.einsum(
        "kgi,gitc->tkc", phase_rows, received, preferred_element_type=jnp.float32
    )
    rows = (2.0 * rows).astype(jnp.bfloat16)

    cycles_here = points_in[0].astype(jnp.int32)
    phis_here = points_in[1].astype(jnp.int32)
    offset_rows = points_in[2] + (points_in[3] + points_in[4])
    offset_cols = points_in[5] + (points_in[6] + points_in[7])
    tap_shift = jnp.arange(TAPS).astype(jnp.float32) - 3.0
    across = kernel_taps(tap_shift[None, :] - offset_rows[:, None])
    beside_all = kernel_taps(tap_shift[None, :] - offset_cols[:, None])
    first_row = (me - 1) * cycle_depth + lead
    cycle_weights = spread_weights(cycles_here - 3 - first_row, across, window)
    phi_weights = spread_weights(phis_here - 3, beside_all, NPHI)
    dense = (cycle_weights[:, :, None] * phi_weights[:, None, :]).astype(jnp.bfloat16)
    values = lax.dot_general(
        dense, rows, (((1, 2), (0, 1)), ((), ())), preferred_element_type=jnp.float32
    )
    values = values.reshape(owner_count, capacity, width_out)
    returned = lax.all_to_all(values, "ma", split_axis=0, concat_axis=0, tiled=True)
    pick = (
        flat_slot[:, None] == jnp.arange(owner_count * capacity, dtype=jnp.int32)[None, :]
    ).astype(jnp.float32)
    return jnp.dot(
        pick,
        returned.reshape(owner_count * capacity, width_out),
        precision=lax.Precision.HIGHEST,
    )


def solution(mesh):
    in_specs = (
        P(("ma", "band"), None, None),
        P(("ma", "band"), None, None, None),
        P(),
        P(("ma", "band")),
        P(("ma", "band")),
        P(None, ("ma", "band")),
    )
    out_specs = P(("ma", "band"), None)
    return jax.shard_map(
        on_device, mesh=mesh, in_specs=in_specs, out_specs=out_specs, check_vma=False
    )
```

```python
import jax
import jax.numpy as jnp
from jax import lax
from jax.sharding import PartitionSpec as P

NPHI = 128
TAPS = 8
FIELDS = 8


def kernel_taps(shifts):
    return jnp.sinc(shifts) * jnp.sinc(shifts / 4.0)


def combine_parts(plus_part, minus_part):
    q_real = -(plus_part[:, 0, 0] - minus_part[:, 1, 1])
    q_imag = -(plus_part[:, 0, 1] + minus_part[:, 1, 0])
    u_real = -(plus_part[:, 1, 0] + minus_part[:, 0, 1])
    u_imag = -(plus_part[:, 1, 1] - minus_part[:, 0, 0])
    real_part = jnp.concatenate([q_real, u_real], axis=1)
    imag_part = jnp.concatenate([q_imag, u_imag], axis=1)
    return jnp.stack([real_part, imag_part], axis=1).astype(jnp.bfloat16)


def phase_table(m_values, cell_count, lmax_width):
    pixel_index = jnp.arange(cell_count, dtype=jnp.int32)
    period = 2 * lmax_width
    phase_turns = m_values[None, :] * pixel_index[:, None] % period
    angles = phase_turns.astype(jnp.float32) * (2.0 * jnp.pi / period)
    return jnp.stack([jnp.cos(angles), -jnp.sin(angles)], axis=-1).astype(jnp.bfloat16)


def spread_weights(starts, weights, length):
    cells = jnp.arange(length, dtype=jnp.int32)[None, :] - starts[:, None]
    spread = jnp.zeros(cells.shape, weights.dtype)
    for tap in range(TAPS):
        spread = spread + jnp.where(cells == tap, weights[:, tap : tap + 1], 0.0)
    return spread


def split_three(x):
    hi = lax.reduce_precision(x, exponent_bits=8, mantissa_bits=7)
    rest = x - hi
    mid = lax.reduce_precision(rest, exponent_bits=8, mantissa_bits=7)
    return hi, mid, rest - mid


def on_device(harmonics, legendre, m_values, cycle_cell, phi_cell, offsets):
    evolutions = harmonics.shape[2] // 4
    cycle_total = legendre.shape[3]
    owner_count = lax.axis_size("ma")
    band_count = lax.axis_size("band")
    blocks = owner_count * band_count
    cycle_depth = cycle_total // blocks
    window = 3 * cycle_depth
    lead = 1
    capacity = cycle_cell.shape[0] // 8
    me = lax.axis_index("ma")
    my_band = lax.axis_index("band")

    both = lax.dot_general(
        legendre[0], harmonics[0], (((1,), (0,)), ((), ())), preferred_element_type=jnp.float32
    )
    spectra = combine_parts(
        both[0].reshape(cycle_total, 2, 2, evolutions),
        both[1].reshape(cycle_total, 2, 2, evolutions),
    )
    width_out = spectra.shape[2]
    by_band = spectra.reshape(owner_count, band_count, cycle_depth, 2, width_out)
    by_band = by_band.transpose(1, 0, 2, 3, 4)
    empty = jnp.zeros((band_count, 1, cycle_depth, 2, width_out), spectra.dtype)
    padded = jnp.concatenate([empty, by_band, empty], axis=1)
    windows = jnp.stack(
        [padded[:, s : s + owner_count] for s in range(3)], axis=2
    )
    windows = windows.transpose(1, 0, 4, 2, 3, 5).reshape(blocks, 2, window, width_out)

    owner_index = cycle_cell // cycle_depth
    one_hot = (owner_index[:, None] == jnp.arange(owner_count, dtype=jnp.int32)[None, :]).astype(
        jnp.int32
    )
    slot_index = jnp.sum((jnp.cumsum(one_hot, axis=0) - one_hot) * one_hot, axis=1)
    flat_slot = owner_index * capacity + slot_index
    placement = (
        flat_slot[:, None] == jnp.arange(owner_count * capacity, dtype=jnp.int32)[None, :]
    ).astype(jnp.bfloat16)
    table = jnp.stack(
        [cycle_cell.astype(jnp.float32), phi_cell.astype(jnp.float32)]
        + list(split_three(offsets[0]))
        + list(split_three(offsets[1])),
        axis=1,
    ).astype(jnp.bfloat16)
    payload = jnp.dot(table.T, placement, preferred_element_type=jnp.float32)
    payload = payload.astype(jnp.bfloat16).reshape(FIELDS, owner_count, capacity)
    payload = payload.transpose(1, 0, 2).reshape(owner_count, 1, 1, 1, capacity * FIELDS)
    payload = jnp.broadcast_to(payload, (owner_count, band_count, 1, 1, capacity * FIELDS))
    payload = payload.reshape(blocks, 1, 1, capacity * FIELDS)
    payload = jnp.concatenate([payload, jnp.zeros_like(payload)], axis=1)
    send = windows.at[:, :, :lead].set(payload)
    received = lax.all_to_all(send, ("ma", "band"), split_axis=0, concat_axis=0, tiled=True)

    points_in = received[:, 0, 0].reshape(owner_count, band_count, capacity * FIELDS)
    points_in = lax.dynamic_index_in_dim(points_in, my_band, axis=1, keepdims=False)
    points_in = points_in.reshape(owner_count, FIELDS, capacity).transpose(1, 0, 2)
    points_in = points_in.reshape(FIELDS, owner_count * capacity).astype(jnp.float32)

    phase_rows = phase_table(m_values, NPHI, harmonics.shape[1])
    rows = jnp.einsum(
        "kgi,gitc->tkc", phase_rows, received, preferred_element_type=jnp.float32
    )
    rows = (2.0 * rows).astype(jnp.bfloat16)

    cycles_here = points_in[0].astype(jnp.int32)
    phis_here = points_in[1].astype(jnp.int32)
    offset_rows = points_in[2] + (points_in[3] + points_in[4])
    offset_cols = points_in[5] + (points_in[6] + points_in[7])
    tap_shift = jnp.arange(TAPS).astype(jnp.float32) - 3.0
    across = kernel_taps(tap_shift[None, :] - offset_rows[:, None])
    beside_all = kernel_taps(tap_shift[None, :] - offset_cols[:, None])
    first_row = (me - 1) * cycle_depth
    cycle_weights = spread_weights(cycles_here - 3 - first_row, across, window)
    phi_weights = spread_weights(phis_here - 3, beside_all, NPHI)
    dense = (cycle_weights[:, :, None] * phi_weights[:, None, :]).astype(jnp.bfloat16)
    values = lax.dot_general(
        dense, rows, (((1, 2), (0, 1)), ((), ())), preferred_element_type=jnp.float32
    )
    values = values.reshape(owner_count, capacity, width_out)
    returned = lax.all_to_all(values, "ma", split_axis=0, concat_axis=0, tiled=True)
    pick = (
        flat_slot[:, None] == jnp.arange(owner_count * capacity, dtype=jnp.int32)[None, :]
    ).astype(jnp.float32)
    return jnp.dot(
        pick,
        returned.reshape(owner_count * capacity, width_out),
        precision=lax.Precision.HIGHEST,
    )


def solution(mesh):
    in_specs = (
        P(("ma", "band"), None, None),
        P(("ma", "band"), None, None, None),
        P(),
        P(("ma", "band")),
        P(("ma", "band")),
        P(None, ("ma", "band")),
    )
    out_specs = P(("ma", "band"), None)
    return jax.shard_map(
        on_device, mesh=mesh, in_specs=in_specs, out_specs=out_specs, check_vma=False
    )
```

```python
import jax
import jax.numpy as jnp
from jax import lax
from jax.experimental.layout import Layout, with_layout_constraint
from jax.sharding import PartitionSpec as P

NPHI = 128
TAPS = 8
FIELDS = 8


def kernel_taps(shifts):
    return jnp.sinc(shifts) * jnp.sinc(shifts / 4.0)


def combine_parts(plus_part, minus_part):
    q_real = -(plus_part[:, 0, 0] - minus_part[:, 1, 1])
    q_imag = -(plus_part[:, 0, 1] + minus_part[:, 1, 0])
    u_real = -(plus_part[:, 1, 0] + minus_part[:, 0, 1])
    u_imag = -(plus_part[:, 1, 1] - minus_part[:, 0, 0])
    real_part = jnp.concatenate([q_real, u_real], axis=1)
    imag_part = jnp.concatenate([q_imag, u_imag], axis=1)
    return jnp.stack([real_part, imag_part], axis=1).astype(jnp.bfloat16)


def phase_table(m_values, cell_count, lmax_width):
    pixel_index = jnp.arange(cell_count, dtype=jnp.int32)
    period = 2 * lmax_width
    phase_turns = m_values[None, :] * pixel_index[:, None] % period
    angles = phase_turns.astype(jnp.float32) * (2.0 * jnp.pi / period)
    return jnp.stack([jnp.cos(angles), -jnp.sin(angles)], axis=-1).astype(jnp.bfloat16)


def spread_weights(starts, weights, length):
    cells = jnp.arange(length, dtype=jnp.int32)[None, :] - starts[:, None]
    spread = jnp.zeros(cells.shape, weights.dtype)
    for tap in range(TAPS):
        spread = spread + jnp.where(cells == tap, weights[:, tap : tap + 1], 0.0)
    return spread


def split_three(x):
    hi = lax.reduce_precision(x, exponent_bits=8, mantissa_bits=7)
    rest = x - hi
    mid = lax.reduce_precision(rest, exponent_bits=8, mantissa_bits=7)
    return hi, mid, rest - mid


def on_device(harmonics, legendre, m_values, cycle_cell, phi_cell, offsets):
    evolutions = harmonics.shape[2] // 4
    cycle_total = legendre.shape[3]
    owner_count = lax.axis_size("ma")
    band_count = lax.axis_size("band")
    blocks = owner_count * band_count
    cycle_depth = cycle_total // blocks
    window = 3 * cycle_depth
    lead = 1
    capacity = cycle_cell.shape[0] // 8
    me = lax.axis_index("ma")
    my_band = lax.axis_index("band")

    both = lax.dot_general(
        legendre[0], harmonics[0], (((1,), (0,)), ((), ())), preferred_element_type=jnp.float32
    )
    both = with_layout_constraint(both, Layout(major_to_minor=(0, 1, 2)))
    spectra = combine_parts(
        both[0].reshape(cycle_total, 2, 2, evolutions),
        both[1].reshape(cycle_total, 2, 2, evolutions),
    )
    width_out = spectra.shape[2]
    by_band = spectra.reshape(owner_count, band_count, cycle_depth, 2, width_out)
    by_band = by_band.transpose(1, 0, 2, 3, 4)
    empty = jnp.zeros((band_count, 1, cycle_depth, 2, width_out), spectra.dtype)
    padded = jnp.concatenate([empty, by_band, empty], axis=1)
    windows = jnp.stack(
        [padded[:, s : s + owner_count] for s in range(3)], axis=2
    )
    windows = windows.transpose(1, 0, 4, 2, 3, 5).reshape(blocks, 2, window, width_out)

    owner_index = cycle_cell // cycle_depth
    one_hot = (owner_index[:, None] == jnp.arange(owner_count, dtype=jnp.int32)[None, :]).astype(
        jnp.int32
    )
    slot_index = jnp.sum((jnp.cumsum(one_hot, axis=0) - one_hot) * one_hot, axis=1)
    flat_slot = owner_index * capacity + slot_index
    placement = (
        flat_slot[:, None] == jnp.arange(owner_count * capacity, dtype=jnp.int32)[None, :]
    ).astype(jnp.bfloat16)
    table = jnp.stack(
        [cycle_cell.astype(jnp.float32), phi_cell.astype(jnp.float32)]
        + list(split_three(offsets[0]))
        + list(split_three(offsets[1])),
        axis=1,
    ).astype(jnp.bfloat16)
    payload = jnp.dot(table.T, placement, preferred_element_type=jnp.float32)
    payload = payload.astype(jnp.bfloat16).reshape(FIELDS, owner_count, capacity)
    payload = payload.transpose(1, 0, 2).reshape(owner_count, 1, 1, 1, capacity * FIELDS)
    payload = jnp.broadcast_to(payload, (owner_count, band_count, 1, 1, capacity * FIELDS))
    payload = payload.reshape(blocks, 1, 1, capacity * FIELDS)
    payload = jnp.concatenate([payload, jnp.zeros_like(payload)], axis=1)
    send = windows.at[:, :, :lead].set(payload)
    received = lax.all_to_all(send, ("ma", "band"), split_axis=0, concat_axis=0, tiled=True)

    points_in = received[:, 0, 0].reshape(owner_count, band_count, capacity * FIELDS)
    points_in = lax.dynamic_index_in_dim(points_in, my_band, axis=1, keepdims=False)
    points_in = points_in.reshape(owner_count, FIELDS, capacity).transpose(1, 0, 2)
    points_in = points_in.reshape(FIELDS, owner_count * capacity).astype(jnp.float32)

    phase_rows = phase_table(m_values, NPHI, harmonics.shape[1])
    rows = jnp.einsum(
        "kgi,gitc->tkc", phase_rows, received, preferred_element_type=jnp.float32
    )
    rows = (2.0 * rows).astype(jnp.bfloat16)

    cycles_here = points_in[0].astype(jnp.int32)
    phis_here = points_in[1].astype(jnp.int32)
    offset_rows = points_in[2] + (points_in[3] + points_in[4])
    offset_cols = points_in[5] + (points_in[6] + points_in[7])
    tap_shift = jnp.arange(TAPS).astype(jnp.float32) - 3.0
    across = kernel_taps(tap_shift[None, :] - offset_rows[:, None])
    beside_all = kernel_taps(tap_shift[None, :] - offset_cols[:, None])
    first_row = (me - 1) * cycle_depth
    cycle_weights = spread_weights(cycles_here - 3 - first_row, across, window)
    phi_weights = spread_weights(phis_here - 3, beside_all, NPHI)
    dense = (cycle_weights[:, :, None] * phi_weights[:, None, :]).astype(jnp.bfloat16)
    values = lax.dot_general(
        dense, rows, (((1, 2), (0, 1)), ((), ())), preferred_element_type=jnp.float32
    )
    values = values.reshape(owner_count, capacity, width_out)
    returned = lax.all_to_all(values, "ma", split_axis=0, concat_axis=0, tiled=True)
    pick = (
        flat_slot[:, None] == jnp.arange(owner_count * capacity, dtype=jnp.int32)[None, :]
    ).astype(jnp.float32)
    return jnp.dot(
        pick,
        returned.reshape(owner_count * capacity, width_out),
        precision=lax.Precision.HIGHEST,
    )


def solution(mesh):
    in_specs = (
        P(("ma", "band"), None, None),
        P(("ma", "band"), None, None, None),
        P(),
        P(("ma", "band")),
        P(("ma", "band")),
        P(None, ("ma", "band")),
    )
    out_specs = P(("ma", "band"), None)
    return jax.shard_map(
        on_device, mesh=mesh, in_specs=in_specs, out_specs=out_specs, check_vma=False
    )
```

```python
import jax
import jax.numpy as jnp
from jax import lax
from jax.experimental.layout import Layout, with_layout_constraint
from jax.sharding import PartitionSpec as P

NPHI = 128
TAPS = 8
FIELDS = 8


def kernel_taps(shifts):
    return jnp.sinc(shifts) * jnp.sinc(shifts / 4.0)


def combine_parts(plus_part, minus_part):
    q_real = -(plus_part[:, 0, 0] - minus_part[:, 1, 1])
    q_imag = -(plus_part[:, 0, 1] + minus_part[:, 1, 0])
    u_real = -(plus_part[:, 1, 0] + minus_part[:, 0, 1])
    u_imag = -(plus_part[:, 1, 1] - minus_part[:, 0, 0])
    real_part = jnp.concatenate([q_real, u_real], axis=1)
    imag_part = jnp.concatenate([q_imag, u_imag], axis=1)
    return jnp.stack([real_part, imag_part], axis=1).astype(jnp.bfloat16)


def phase_table(m_values, cell_count, lmax_width):
    pixel_index = jnp.arange(cell_count, dtype=jnp.int32)
    period = 2 * lmax_width
    phase_turns = m_values[None, :] * pixel_index[:, None] % period
    angles = phase_turns.astype(jnp.float32) * (2.0 * jnp.pi / period)
    return jnp.stack([jnp.cos(angles), -jnp.sin(angles)], axis=-1).astype(jnp.bfloat16)


def spread_weights(starts, weights, length):
    cells = jnp.arange(length, dtype=jnp.int32)[None, :] - starts[:, None]
    spread = jnp.zeros(cells.shape, weights.dtype)
    for tap in range(TAPS):
        spread = spread + jnp.where(cells == tap, weights[:, tap : tap + 1], 0.0)
    return spread


def split_three(x):
    hi = lax.reduce_precision(x, exponent_bits=8, mantissa_bits=7)
    rest = x - hi
    mid = lax.reduce_precision(rest, exponent_bits=8, mantissa_bits=7)
    return hi, mid, rest - mid


def on_device(harmonics, legendre, m_values, cycle_cell, phi_cell, offsets):
    evolutions = harmonics.shape[2] // 4
    cycle_total = legendre.shape[3]
    owner_count = lax.axis_size("ma")
    band_count = lax.axis_size("band")
    blocks = owner_count * band_count
    cycle_depth = cycle_total // blocks
    window = 3 * cycle_depth
    lead = 1
    capacity = cycle_cell.shape[0] // 8
    me = lax.axis_index("ma")
    my_band = lax.axis_index("band")

    both = lax.dot_general(
        legendre[0], harmonics[0], (((1,), (0,)), ((), ())), preferred_element_type=jnp.float32
    )
    both = with_layout_constraint(both, Layout(major_to_minor=(0, 1, 2)))
    spectra = combine_parts(
        both[0].reshape(cycle_total, 2, 2, evolutions),
        both[1].reshape(cycle_total, 2, 2, evolutions),
    )
    width_out = spectra.shape[2]
    by_band = spectra.reshape(owner_count, band_count, cycle_depth, 2, width_out)
    by_band = by_band.transpose(1, 0, 2, 3, 4)
    empty = jnp.zeros((band_count, 1, cycle_depth, 2, width_out), spectra.dtype)
    padded = jnp.concatenate([empty, by_band, empty], axis=1)
    windows = jnp.stack(
        [padded[:, s : s + owner_count] for s in range(3)], axis=2
    )
    windows = windows.transpose(1, 0, 4, 2, 3, 5).reshape(blocks, 2, window, width_out)

    owner_index = cycle_cell // cycle_depth
    one_hot = (owner_index[:, None] == jnp.arange(owner_count, dtype=jnp.int32)[None, :]).astype(
        jnp.int32
    )
    slot_index = jnp.sum((jnp.cumsum(one_hot, axis=0) - one_hot) * one_hot, axis=1)
    flat_slot = owner_index * capacity + slot_index
    placement = (
        flat_slot[:, None] == jnp.arange(owner_count * capacity, dtype=jnp.int32)[None, :]
    ).astype(jnp.bfloat16)
    table = jnp.stack(
        [cycle_cell.astype(jnp.float32), phi_cell.astype(jnp.float32)]
        + list(split_three(offsets[0]))
        + list(split_three(offsets[1])),
        axis=1,
    ).astype(jnp.bfloat16)
    payload = jnp.dot(table.T, placement, preferred_element_type=jnp.float32)
    payload = payload.astype(jnp.bfloat16).reshape(FIELDS, owner_count, capacity)
    payload = payload.transpose(1, 0, 2).reshape(owner_count, 1, 1, 1, capacity * FIELDS)
    payload = jnp.broadcast_to(payload, (owner_count, band_count, 1, 1, capacity * FIELDS))
    payload = payload.reshape(blocks, 1, 1, capacity * FIELDS)
    payload = jnp.concatenate([payload, jnp.zeros_like(payload)], axis=1)
    send = windows.at[:, :, :lead].set(payload)
    received = lax.all_to_all(send, ("ma", "band"), split_axis=0, concat_axis=0, tiled=True)

    points_in = received[:, 0, 0].reshape(owner_count, band_count, capacity * FIELDS)
    points_in = lax.dynamic_index_in_dim(points_in, my_band, axis=1, keepdims=False)
    points_in = points_in.reshape(owner_count, FIELDS, capacity).transpose(1, 0, 2)
    points_in = points_in.reshape(FIELDS, owner_count * capacity).astype(jnp.float32)

    phase_rows = phase_table(m_values, NPHI, harmonics.shape[1])
    rows = jnp.einsum(
        "kgi,gitc->tkc", phase_rows, received, preferred_element_type=jnp.float32
    )
    rows = (2.0 * rows).astype(jnp.bfloat16)

    cycles_here = points_in[0].astype(jnp.int32)
    phis_here = points_in[1].astype(jnp.int32)
    offset_rows = points_in[2] + (points_in[3] + points_in[4])
    offset_cols = points_in[5] + (points_in[6] + points_in[7])
    tap_shift = jnp.arange(TAPS).astype(jnp.float32) - 3.0
    across = kernel_taps(tap_shift[None, :] - offset_rows[:, None])
    beside_all = kernel_taps(tap_shift[None, :] - offset_cols[:, None])
    first_row = (me - 1) * cycle_depth
    cycle_weights = spread_weights(cycles_here - 3 - first_row, across, window)
    phi_weights = spread_weights(phis_here - 3, beside_all, NPHI)
    dense = (cycle_weights[:, :, None] * phi_weights[:, None, :]).astype(jnp.bfloat16)
    values = lax.dot_general(
        dense, rows, (((1, 2), (0, 1)), ((), ())), preferred_element_type=jnp.float32
    )
    values = values.reshape(owner_count, capacity, width_out)
    returned = lax.all_to_all(values, "ma", split_axis=0, concat_axis=0, tiled=True)
    pick = (
        flat_slot[:, None] == jnp.arange(owner_count * capacity, dtype=jnp.int32)[None, :]
    ).astype(jnp.float32)
    return jnp.dot(
        pick,
        returned.reshape(owner_count * capacity, width_out),
        precision=lax.Precision.HIGH,
    )


def solution(mesh):
    in_specs = (
        P(("ma", "band"), None, None),
        P(("ma", "band"), None, None, None),
        P(),
        P(("ma", "band")),
        P(("ma", "band")),
        P(None, ("ma", "band")),
    )
    out_specs = P(("ma", "band"), None)
    return jax.shard_map(
        on_device, mesh=mesh, in_specs=in_specs, out_specs=out_specs, check_vma=False
    )
```

```python
import jax
import jax.numpy as jnp
from jax import lax
from jax.experimental.layout import Layout, with_layout_constraint
from jax.sharding import PartitionSpec as P

NPHI = 128
TAPS = 8
FIELDS = 8


def kernel_taps(shifts):
    return jnp.sinc(shifts) * jnp.sinc(shifts / 4.0)


def combine_parts(plus_part, minus_part):
    q_real = -(plus_part[:, 0, 0] - minus_part[:, 1, 1])
    q_imag = -(plus_part[:, 0, 1] + minus_part[:, 1, 0])
    u_real = -(plus_part[:, 1, 0] + minus_part[:, 0, 1])
    u_imag = -(plus_part[:, 1, 1] - minus_part[:, 0, 0])
    real_part = jnp.concatenate([q_real, u_real], axis=1)
    imag_part = jnp.concatenate([q_imag, u_imag], axis=1)
    return jnp.stack([real_part, imag_part], axis=1).astype(jnp.bfloat16)


def phase_table(m_values, cell_count, lmax_width):
    pixel_index = jnp.arange(cell_count, dtype=jnp.int32)
    period = 2 * lmax_width
    phase_turns = m_values[None, :] * pixel_index[:, None] % period
    angles = phase_turns.astype(jnp.float32) * (2.0 * jnp.pi / period)
    return jnp.stack([jnp.cos(angles), -jnp.sin(angles)], axis=-1).astype(jnp.bfloat16)


def spread_weights(starts, weights, length):
    cells = jnp.arange(length, dtype=jnp.int32)[None, :] - starts[:, None]
    spread = jnp.zeros(cells.shape, weights.dtype)
    for tap in range(TAPS):
        spread = spread + jnp.where(cells == tap, weights[:, tap : tap + 1], 0.0)
    return spread


def split_three(x):
    hi = lax.reduce_precision(x, exponent_bits=8, mantissa_bits=7)
    rest = x - hi
    mid = lax.reduce_precision(rest, exponent_bits=8, mantissa_bits=7)
    return hi, mid, rest - mid


def on_device(harmonics, legendre, m_values, cycle_cell, phi_cell, offsets):
    evolutions = harmonics.shape[2] // 4
    cycle_total = legendre.shape[3]
    owner_count = lax.axis_size("ma")
    band_count = lax.axis_size("band")
    blocks = owner_count * band_count
    cycle_depth = cycle_total // blocks
    window = 3 * cycle_depth
    lead = 1
    capacity = cycle_cell.shape[0] // 8
    me = lax.axis_index("ma")
    my_band = lax.axis_index("band")

    both = lax.dot_general(
        legendre[0], harmonics[0], (((1,), (0,)), ((), ())), preferred_element_type=jnp.float32
    )
    both = with_layout_constraint(both, Layout(major_to_minor=(0, 1, 2)))
    spectra = combine_parts(
        both[0].reshape(cycle_total, 2, 2, evolutions),
        both[1].reshape(cycle_total, 2, 2, evolutions),
    )
    width_out = spectra.shape[2]
    by_band = spectra.reshape(owner_count, band_count, cycle_depth, 2, width_out)
    by_band = by_band.transpose(1, 0, 2, 3, 4)
    empty = jnp.zeros((band_count, 1, cycle_depth, 2, width_out), spectra.dtype)
    padded = jnp.concatenate([empty, by_band, empty], axis=1)
    windows = jnp.stack(
        [padded[:, s : s + owner_count] for s in range(3)], axis=2
    )
    windows = windows.transpose(1, 0, 4, 2, 3, 5).reshape(blocks, 2, window, width_out)

    owner_index = cycle_cell // cycle_depth
    one_hot = (owner_index[:, None] == jnp.arange(owner_count, dtype=jnp.int32)[None, :]).astype(
        jnp.int32
    )
    slot_index = jnp.sum((jnp.cumsum(one_hot, axis=0) - one_hot) * one_hot, axis=1)
    flat_slot = owner_index * capacity + slot_index
    placement = (
        flat_slot[:, None] == jnp.arange(owner_count * capacity, dtype=jnp.int32)[None, :]
    ).astype(jnp.bfloat16)
    table = jnp.stack(
        [cycle_cell.astype(jnp.float32), phi_cell.astype(jnp.float32)]
        + list(split_three(offsets[0]))
        + list(split_three(offsets[1])),
        axis=1,
    ).astype(jnp.bfloat16)
    payload = jnp.dot(table.T, placement, preferred_element_type=jnp.float32)
    payload = payload.astype(jnp.bfloat16).reshape(FIELDS, owner_count, capacity)
    payload = payload.transpose(1, 0, 2).reshape(owner_count, 1, 1, 1, capacity * FIELDS)
    payload = jnp.broadcast_to(payload, (owner_count, band_count, 1, 1, capacity * FIELDS))
    payload = payload.reshape(blocks, 1, 1, capacity * FIELDS)
    send = windows.at[:, :1, :lead].set(payload)
    received = lax.all_to_all(send, ("ma", "band"), split_axis=0, concat_axis=0, tiled=True)

    points_in = received[:, 0, 0].reshape(owner_count, band_count, capacity * FIELDS)
    points_in = lax.dynamic_index_in_dim(points_in, my_band, axis=1, keepdims=False)
    points_in = points_in.reshape(owner_count, FIELDS, capacity).transpose(1, 0, 2)
    points_in = points_in.reshape(FIELDS, owner_count * capacity).astype(jnp.float32)

    phase_rows = phase_table(m_values, NPHI, harmonics.shape[1])
    rows = jnp.einsum(
        "kgi,gitc->tkc", phase_rows, received, preferred_element_type=jnp.float32
    )
    rows = (2.0 * rows).astype(jnp.bfloat16)

    cycles_here = points_in[0].astype(jnp.int32)
    phis_here = points_in[1].astype(jnp.int32)
    offset_rows = points_in[2] + (points_in[3] + points_in[4])
    offset_cols = points_in[5] + (points_in[6] + points_in[7])
    tap_shift = jnp.arange(TAPS).astype(jnp.float32) - 3.0
    across = kernel_taps(tap_shift[None, :] - offset_rows[:, None])
    beside_all = kernel_taps(tap_shift[None, :] - offset_cols[:, None])
    first_row = (me - 1) * cycle_depth
    cycle_weights = spread_weights(cycles_here - 3 - first_row, across, window)
    phi_weights = spread_weights(phis_here - 3, beside_all, NPHI)
    dense = (cycle_weights[:, :, None] * phi_weights[:, None, :]).astype(jnp.bfloat16)
    values = lax.dot_general(
        dense, rows, (((1, 2), (0, 1)), ((), ())), preferred_element_type=jnp.float32
    )
    values = values.reshape(owner_count, capacity, width_out)
    returned = lax.all_to_all(values, "ma", split_axis=0, concat_axis=0, tiled=True)
    pick = (
        flat_slot[:, None] == jnp.arange(owner_count * capacity, dtype=jnp.int32)[None, :]
    ).astype(jnp.float32)
    return jnp.dot(
        pick,
        returned.reshape(owner_count * capacity, width_out),
        precision=lax.Precision.HIGHEST,
    )


def solution(mesh):
    in_specs = (
        P(("ma", "band"), None, None),
        P(("ma", "band"), None, None, None),
        P(),
        P(("ma", "band")),
        P(("ma", "band")),
        P(None, ("ma", "band")),
    )
    out_specs = P(("ma", "band"), None)
    return jax.shard_map(
        on_device, mesh=mesh, in_specs=in_specs, out_specs=out_specs, check_vma=False
    )
```
